32 devices in a mesh: groups: 2 (over y), tile: 4 (over z), chan: 2 (over x), low: 2 (over core).
Axes of the slice: x: 2, y: 2, z: 4, core: 2. Of those that a mesh axis runs over, the one named last changes fastest.
Arguments:
- latent_map: bfloat16 [16, 16, 16, 512], P('groups', 'tile', 'chan'), parts along dimension 0, may hold values from -6 to 6
- inner_map: bfloat16 [16, 16, 16, 512], P(('groups', 'tile'), None, 'chan'), parts along dimension 0, may hold values from -6 to 6
- timestep: int32 [16], P('groups'), parts along dimension 0, may hold values from 0 to 999
- conv_weight: bfloat16 [3, 3, 512, 512], P(None, None, None, 'low'), may hold values from -0.09375 to 0.09375
- time_weight: bfloat16 [256, 512], P(None, 'low'), may hold values from -0.375 to 0.375
- attend_weight: bfloat16 [3, 512, 512], P(None, None, 'low'), may hold values from -8 to 8
Outputs:
- attended: bfloat16 [16, 16, 16, 512], P(('groups', 'tile'), None, 'chan', 'low'), parts along dimension 0
The draws below stay inside these ranges and needn't reach their ends.
There are 2 independent parts, one for each index of `groups`. The reference program is written for one: setup_inputs(seed, part) draws one part's arguments, and reference() takes and returns one part's arrays. A program takes and returns all parts, laid end to end along the dimension named above; an argument that names none is the same for every part. Nothing has to cross between parts.
All inputs are finite; a program needn't handle non-finite values.
Results may differ from the reference program's by a relative error of at most 0.017.
The reference program's roundings to bfloat16 on the way (of `joined`, `features`, `projections` and `rounded`) count: a program that leaves them out, or rounds other values in their place, can miss the bound.
Values may be sent and summed in bfloat16 or wider, within the bound.
No kernel may reach another device: no remote copies, remote signals or barrier semaphores. Data moves between devices by JAX's collectives and lax.ppermute only.
A program may use at most 64 MiB of HBM per device.

```python
import math
import jax
import jax.numpy as jnp
from jax import lax

C = 512
HEAD = 64
TE = 256
B = 8
R = 16
W = 16


def draw_attend_weight(key, part):
    standard = jax.random.truncated_normal(jax.random.fold_in(key, 11), -4.0, 4.0, (3, C, C), jnp.float32) / math.sqrt(C)
    head_count = C // HEAD
    strength = jax.random.uniform(jax.random.fold_in(key, 12), (head_count,), jnp.float32, 1.5, 2.5)
    query_factor = jnp.repeat(strength, HEAD)
    factor = jnp.concatenate([query_factor[None, :], jnp.ones((2, C), jnp.float32)], axis=0)
    return jnp.clip(standard * factor[:, None, :], -8.0, 8.0).astype(jnp.bfloat16)


def plant(drawn, stream_key, least, high):
    index_at = [jax.random.randint(jax.random.fold_in(stream_key, axis), (), 0, length) for axis, length in enumerate(drawn.shape)]
    widest = drawn.shape.index(max(drawn.shape))
    beside = index_at[:widest] + [(index_at[widest] + 1) % drawn.shape[widest]] + index_at[widest + 1:]
    return drawn.at[tuple(index_at)].set(least).at[tuple(beside)].set(high)


def block_scale(key, dims, split, least, top_value):
    loudness = 1.0
    for dim, parts in split:
        draws = jax.random.uniform(jax.random.fold_in(jax.random.fold_in(key, 6), dim), (parts,), jnp.float32, least / len(split), top_value / len(split))
        loudness = loudness * jnp.repeat(jnp.exp(draws), dims[dim] // parts).reshape((-1,) + (1,) * (len(dims) - 1 - dim))
    return loudness


def bell_draw(stream_key, dims, scale, most, shards=(), held_as=jnp.bfloat16):
    factor_of = block_scale(stream_key, dims, shards, -0.22, 0.18) if shards else 1.0
    drawn = jax.random.normal(stream_key, dims, jnp.float32) * scale * factor_of
    return jnp.minimum(jnp.maximum(drawn, -most), most).astype(held_as)


def setup_inputs(seed: int = 0, part: int = 0) -> dict:
    keys = jax.random.split(jax.random.key(seed), 7)
    part_keys = jax.random.split(jax.random.fold_in(keys[6], part), 7)
    return {
        "latent_map": bell_draw(part_keys[0], (B, R, W, C), 1.0, 6.0, ((1, 4), (2, 2))),
        "inner_map": bell_draw(part_keys[1], (B, R, W, C), 1.0, 6.0, ((0, 4), (2, 2))),
        "timestep": plant(jax.random.randint(part_keys[2], (B,), 0, 1000), jax.random.fold_in(part_keys[2], 1), 0, 999).astype(jnp.int32),
        "conv_weight": bell_draw(keys[3], (3, 3, C, C), (9 * C) ** -0.5, 0.09375, ((3, 2),)),
        "time_weight": bell_draw(keys[4], (TE, C), TE ** -0.5, 0.375, ((1, 2),)),
        "attend_weight": draw_attend_weight(jax.random.fold_in(keys[6], 71), part),
    }


def time_embedding(timestep):
    halfway = TE // 2
    ladder = jnp.arange(halfway, dtype=jnp.float32)
    frequency = jnp.exp(ladder * (-math.log(10000.0) / halfway))
    angles = timestep.astype(jnp.float32)[:, None] * frequency[None, :]
    return jnp.concatenate([jnp.sin(angles), jnp.cos(angles)], axis=1)


def convolve(padded, conv_weight, row_count, col_count):
    samples = padded.shape[0]
    positions = samples * row_count * col_count
    summed = jnp.zeros((positions, conv_weight.shape[3]), jnp.float32)
    for row_shift in range(3):
        for col_shift in range(3):
            window = padded[:, row_shift:row_shift + row_count, col_shift:col_shift + col_count, :]
            summed = summed + jnp.dot(window.reshape(positions, padded.shape[3]), conv_weight[row_shift, col_shift], preferred_element_type=jnp.float32)
    return summed.reshape(samples, row_count, col_count, conv_weight.shape[3])


def reference(latent_map, inner_map, timestep, conv_weight, time_weight, attend_weight):
    joined = (latent_map.astype(jnp.float32) + inner_map.astype(jnp.float32)).astype(jnp.bfloat16)
    modulation = jnp.dot(time_embedding(timestep), time_weight.astype(jnp.float32), precision=lax.Precision.HIGHEST)
    padded = jnp.pad(joined, ((0, 0), (1, 1), (1, 1), (0, 0)))
    convolved = convolve(padded, conv_weight, R, W)
    features = jax.nn.silu(convolved * (1.0 + modulation[:, None, None, :])).astype(jnp.bfloat16)
    flattened = features.reshape(B, R * W, C)
    heads_all = C // HEAD

    def one_head(triple):
        query_head, key_head, value_head = triple
        scores = jnp.dot(query_head, key_head.T, preferred_element_type=jnp.float32) * (HEAD ** -0.5)
        row_peak = jnp.max(scores, axis=1, keepdims=True)
        weights = jnp.exp(scores - row_peak)
        totals = jnp.sum(weights, axis=1, keepdims=True)
        rounded = weights.astype(jnp.bfloat16)
        return jnp.dot(rounded, value_head, preferred_element_type=jnp.float32) / totals

    def one_sample(sample):
        projections = [jnp.dot(sample, attend_weight[which], preferred_element_type=jnp.float32).astype(jnp.bfloat16) for which in range(3)]
        by_head = [projection.reshape(R * W, heads_all, HEAD).transpose(1, 0, 2) for projection in projections]
        heads_out = lax.map(one_head, (by_head[0], by_head[1], by_head[2]))
        return heads_out.transpose(1, 0, 2).reshape(R * W, C).astype(jnp.bfloat16)

    attended = lax.map(one_sample, flattened)
    return attended.reshape(B, R, W, C)
```

```python
import math

import jax
import jax.numpy as jnp
from jax import lax
from jax.sharding import PartitionSpec as P

HEAD = 64
TE = 256


def time_embedding(timestep):
    halfway = TE // 2
    ladder = jnp.arange(halfway, dtype=jnp.float32)
    frequency = jnp.exp(ladder * (-math.log(10000.0) / halfway))
    angles = timestep.astype(jnp.float32)[:, None] * frequency[None, :]
    return jnp.concatenate([jnp.sin(angles), jnp.cos(angles)], axis=1)


def swap(tree, axis):
    return lax.ppermute(tree, axis, [(0, 1), (1, 0)])


def convolve(joined, weight):
    return lax.conv_general_dilated(
        joined,
        weight,
        window_strides=(1, 1),
        padding=((1, 1), (1, 1)),
        dimension_numbers=("NHWC", "HWIO", "NHWC"),
        preferred_element_type=jnp.float32,
    )


def attend(queries, keys, values):
    scores = jnp.einsum("nqd,nkd->nqk", queries, keys, preferred_element_type=jnp.float32)
    scores = scores * HEAD ** (-0.5)
    row_peak = jnp.max(scores, axis=2, keepdims=True)
    weights = jnp.exp(scores - row_peak)
    totals = jnp.sum(weights, axis=2, keepdims=True)
    summed = jnp.einsum(
        "nqk,nkd->nqd", weights.astype(jnp.bfloat16), values, preferred_element_type=jnp.float32
    )
    return (summed / totals).astype(jnp.bfloat16)


def per_device(latent_map, inner_map, timestep, conv_weight, time_weight, attend_weight):
    tiles = lax.axis_size("tile")
    lows = lax.axis_size("low")
    t_idx = lax.axis_index("tile")
    c_idx = lax.axis_index("chan")
    l_idx = lax.axis_index("low")
    samples, row_local, col_local, width = latent_map.shape
    per_tile = samples // tiles
    per_core = per_tile // lows
    half = conv_weight.shape[3]
    heads_local = attend_weight.shape[2] // HEAD

    conv_other, time_other = swap((conv_weight, time_weight), "low")

    start = l_idx * per_core
    outgoing = lax.dynamic_slice_in_dim(
        latent_map.reshape(tiles, per_tile, row_local, col_local, width), start, per_core, 1
    ).reshape(tiles * per_core, row_local, col_local, width)
    arrived = lax.all_to_all(outgoing, "tile", split_axis=0, concat_axis=1, tiled=True)
    inner_own = lax.dynamic_slice_in_dim(inner_map, start, per_core, 0)
    joined = (arrived.astype(jnp.float32) + inner_own.astype(jnp.float32)).astype(jnp.bfloat16)
    whole = lax.all_gather(joined, "chan", axis=2, tiled=True)

    stamps = lax.dynamic_slice_in_dim(timestep, t_idx * per_tile + start, per_core, 0)
    embedded = time_embedding(stamps)
    mod_own = jnp.dot(embedded, time_weight.astype(jnp.float32), precision=lax.Precision.HIGHEST)
    mod_other = jnp.dot(embedded, time_other.astype(jnp.float32), precision=lax.Precision.HIGHEST)

    def features_of(weight, modulation):
        convolved = convolve(whole, weight)
        return jax.nn.silu(convolved * (1.0 + modulation[:, None, None, :])).astype(jnp.bfloat16)

    feat_own = features_of(conv_weight, mod_own)
    feat_other = features_of(conv_other, mod_other)
    part_own, part_other = swap((feat_own, feat_other), "low")
    first = l_idx == 0
    half_a = jnp.where(first, jnp.concatenate([feat_own, part_other], 0), jnp.concatenate([part_other, feat_own], 0))
    half_b = jnp.where(first, jnp.concatenate([feat_other, part_own], 0), jnp.concatenate([part_own, feat_other], 0))

    rows_total, cols_total = half_a.shape[1], half_a.shape[2]
    tokens = rows_total * cols_total
    weight_a = lax.dynamic_slice_in_dim(attend_weight, l_idx * half, half, 1)
    weight_b = lax.dynamic_slice_in_dim(attend_weight, (1 - l_idx) * half, half, 1)

    def project(part_a, part_b, which):
        return (
            jnp.dot(part_a, weight_a[which], preferred_element_type=jnp.float32)
            + jnp.dot(part_b, weight_b[which], preferred_element_type=jnp.float32)
        ).astype(jnp.bfloat16)

    col_start = c_idx * col_local
    own_a = lax.dynamic_slice_in_dim(half_a, col_start, col_local, 2)
    own_b = lax.dynamic_slice_in_dim(half_b, col_start, col_local, 2)
    queries = project(own_a.reshape(per_tile, -1, half), own_b.reshape(per_tile, -1, half), 0)
    keys = project(half_a.reshape(per_tile, tokens, half), half_b.reshape(per_tile, tokens, half), 1)
    values = project(half_a.reshape(per_tile, tokens, half), half_b.reshape(per_tile, tokens, half), 2)

    def by_head(x):
        n, k, _ = x.shape
        return x.reshape(n, k, heads_local, HEAD).transpose(0, 2, 1, 3).reshape(n * heads_local, k, HEAD)

    q_heads, k_heads, v_heads = by_head(queries), by_head(keys), by_head(values)
    if tokens * tokens * 4 * q_heads.shape[0] <= (8 << 20):
        out = attend(q_heads, k_heads, v_heads)
    else:
        out = lax.map(lambda trio: attend(*(x[None] for x in trio))[0], (q_heads, k_heads, v_heads))
    out = out.reshape(per_tile, heads_local, row_local * tiles, col_local, HEAD)
    return out.transpose(0, 2, 3, 1, 4).reshape(per_tile, row_local * tiles, col_local, heads_local * HEAD)


def solution(mesh):
    in_specs = (
        P("groups", "tile", "chan", None),
        P(("groups", "tile"), None, "chan", None),
        P("groups"),
        P(None, None, None, "low"),
        P(None, "low"),
        P(None, None, "low"),
    )
    out_specs = P(("groups", "tile"), None, "chan", "low")
    return jax.shard_map(
        per_device, mesh=mesh, in_specs=in_specs, out_specs=out_specs, check_vma=False
    )
```

```python
import math

import jax
import jax.numpy as jnp
from jax import lax
from jax.sharding import PartitionSpec as P

HEAD = 64
TE = 256


def time_embedding(timestep):
    halfway = TE // 2
    ladder = jnp.arange(halfway, dtype=jnp.float32)
    frequency = jnp.exp(ladder * (-math.log(10000.0) / halfway))
    angles = timestep.astype(jnp.float32)[:, None] * frequency[None, :]
    return jnp.concatenate([jnp.sin(angles), jnp.cos(angles)], axis=1)


def swap(tree, axis):
    return lax.ppermute(tree, axis, [(0, 1), (1, 0)])


def gather_map(latent_map, inner_map, start, per_core):
    tiles = lax.axis_size("tile")
    chans = lax.axis_size("chan")
    t_idx = lax.axis_index("tile")
    c_idx = lax.axis_index("chan")
    samples, row_local, col_local, width = latent_map.shape
    per_tile = samples // tiles
    blocks = latent_map.reshape(tiles, per_tile, row_local, col_local, width)
    inner_own = lax.dynamic_slice_in_dim(inner_map, start, per_core, 0)
    if tiles > 4 or chans != 2:
        outgoing = lax.dynamic_slice_in_dim(blocks, start, per_core, 1)
        outgoing = outgoing.reshape(tiles * per_core, row_local, col_local, width)
        arrived = lax.all_to_all(outgoing, "tile", split_axis=0, concat_axis=1, tiled=True)
        joined = (arrived.astype(jnp.float32) + inner_own.astype(jnp.float32)).astype(jnp.bfloat16)
        return lax.all_gather(joined, "chan", axis=2, tiled=True)
    canvas = jnp.zeros((per_core, row_local * tiles, col_local * 2, width), jnp.bfloat16)
    for shift in range(tiles):
        target = (t_idx + shift) % tiles
        chunk = lax.dynamic_slice(
            blocks, (target, start, 0, 0, 0), (1, per_core, row_local, col_local, width)
        )[0]
        if shift:
            chunk = lax.ppermute(chunk, "tile", [(i, (i + shift) % tiles) for i in range(tiles)])
        rows = ((t_idx - shift) % tiles) * row_local
        inner_rows = lax.dynamic_slice_in_dim(inner_own, rows, row_local, 1)
        joined = (chunk.astype(jnp.float32) + inner_rows.astype(jnp.float32)).astype(jnp.bfloat16)
        partner = swap(joined, "chan")
        canvas = lax.dynamic_update_slice(canvas, joined, (0, rows, c_idx * col_local, 0))
        canvas = lax.dynamic_update_slice(canvas, partner, (0, rows, (1 - c_idx) * col_local, 0))
    return canvas


def convolve(joined, weight):
    return lax.conv_general_dilated(
        joined,
        weight,
        window_strides=(1, 1),
        padding=((1, 1), (1, 1)),
        dimension_numbers=("NHWC", "HWIO", "NHWC"),
        preferred_element_type=jnp.float32,
    )


def attend(queries, keys, values):
    scores = jnp.einsum("nqd,nkd->nqk", queries, keys, preferred_element_type=jnp.float32)
    scores = scores * HEAD ** (-0.5)
    row_peak = jnp.max(scores, axis=2, keepdims=True)
    weights = jnp.exp(scores - row_peak)
    totals = jnp.sum(weights, axis=2, keepdims=True)
    summed = jnp.einsum(
        "nqk,nkd->nqd", weights.astype(jnp.bfloat16), values, preferred_element_type=jnp.float32
    )
    return (summed / totals).astype(jnp.bfloat16)


def per_device(latent_map, inner_map, timestep, conv_weight, time_weight, attend_weight):
    tiles = lax.axis_size("tile")
    lows = lax.axis_size("low")
    t_idx = lax.axis_index("tile")
    c_idx = lax.axis_index("chan")
    l_idx = lax.axis_index("low")
    samples, row_local, col_local, width = latent_map.shape
    per_tile = samples // tiles
    per_core = per_tile // lows
    half = conv_weight.shape[3]
    heads_local = attend_weight.shape[2] // HEAD

    conv_other, time_other = swap((conv_weight, time_weight), "low")
    conv_full = lax.dynamic_slice_in_dim(
        jnp.concatenate([conv_weight, conv_other, conv_weight], axis=3), l_idx * half, 2 * half, 3
    )
    time_full = lax.dynamic_slice_in_dim(
        jnp.concatenate([time_weight, time_other, time_weight], axis=1), l_idx * half, 2 * half, 1
    )

    start = l_idx * per_core
    whole = gather_map(latent_map, inner_map, start, per_core)

    stamps = lax.dynamic_slice_in_dim(timestep, t_idx * per_tile + start, per_core, 0)
    modulation = jnp.dot(
        time_embedding(stamps), time_full.astype(jnp.float32), precision=lax.Precision.HIGHEST
    )
    convolved = convolve(whole, conv_full)
    feat_own = jax.nn.silu(convolved * (1.0 + modulation[:, None, None, :])).astype(jnp.bfloat16)
    feat_part = swap(feat_own, "low")
    features = lax.dynamic_slice_in_dim(
        jnp.concatenate([feat_own, feat_part, feat_own], axis=0), l_idx * per_core, per_tile, 0
    )

    rows_total, cols_total = features.shape[1], features.shape[2]
    tokens = rows_total * cols_total

    def project(part, which):
        return jnp.dot(part, attend_weight[which], preferred_element_type=jnp.float32).astype(jnp.bfloat16)

    own_cols = lax.dynamic_slice_in_dim(features, c_idx * col_local, col_local, 2)
    flat = features.reshape(per_tile, tokens, width)
    queries = project(own_cols.reshape(per_tile, -1, width), 0)
    keys = project(flat, 1)
    values = project(flat, 2)

    def by_head(x):
        n, k, _ = x.shape
        return x.reshape(n, k, heads_local, HEAD).transpose(0, 2, 1, 3).reshape(n * heads_local, k, HEAD)

    q_heads, k_heads, v_heads = by_head(queries), by_head(keys), by_head(values)
    if tokens * tokens * 4 * q_heads.shape[0] <= (8 << 20):
        out = attend(q_heads, k_heads, v_heads)
    else:
        out = lax.map(lambda trio: attend(*(x[None] for x in trio))[0], (q_heads, k_heads, v_heads))
    out = out.reshape(per_tile, heads_local, row_local * tiles, col_local, HEAD)
    return out.transpose(0, 2, 3, 1, 4).reshape(per_tile, row_local * tiles, col_local, heads_local * HEAD)


def solution(mesh):
    in_specs = (
        P("groups", "tile", "chan", None),
        P(("groups", "tile"), None, "chan", None),
        P("groups"),
        P(None, None, None, "low"),
        P(None, "low"),
        P(None, None, "low"),
    )
    out_specs = P(("groups", "tile"), None, "chan", "low")
    return jax.shard_map(
        per_device, mesh=mesh, in_specs=in_specs, out_specs=out_specs, check_vma=False
    )
```

```python
import math

import jax
import jax.numpy as jnp
from jax import lax
from jax.sharding import PartitionSpec as P

HEAD = 64
TE = 256


def time_embedding(timestep):
    halfway = TE // 2
    ladder = jnp.arange(halfway, dtype=jnp.float32)
    frequency = jnp.exp(ladder * (-math.log(10000.0) / halfway))
    angles = timestep.astype(jnp.float32)[:, None] * frequency[None, :]
    return jnp.concatenate([jnp.sin(angles), jnp.cos(angles)], axis=1)


def swap(tree, axis):
    return lax.ppermute(tree, axis, [(0, 1), (1, 0)])


def convolve(joined, weight):
    return lax.conv_general_dilated(
        joined,
        weight,
        window_strides=(1, 1),
        padding=((1, 1), (1, 1)),
        dimension_numbers=("NHWC", "HWIO", "NHWC"),
        preferred_element_type=jnp.float32,
    )


def attend(queries, keys, values):
    scores = jnp.einsum("nqd,nkd->nqk", queries, keys, preferred_element_type=jnp.float32)
    scores = scores * HEAD ** (-0.5)
    row_peak = jnp.max(scores, axis=2, keepdims=True)
    weights = jnp.exp(scores - row_peak)
    totals = jnp.sum(weights, axis=2, keepdims=True)
    summed = jnp.einsum(
        "nqk,nkd->nqd", weights.astype(jnp.bfloat16), values, preferred_element_type=jnp.float32
    )
    return (summed / totals).astype(jnp.bfloat16)


def per_device(latent_map, inner_map, timestep, conv_weight, time_weight, attend_weight):
    tiles = lax.axis_size("tile")
    lows = lax.axis_size("low")
    t_idx = lax.axis_index("tile")
    c_idx = lax.axis_index("chan")
    l_idx = lax.axis_index("low")
    samples, row_local, col_local, width = latent_map.shape
    per_tile = samples // tiles
    per_core = per_tile // lows
    half = conv_weight.shape[3]
    heads_local = attend_weight.shape[2] // HEAD

    conv_other, time_other = swap((conv_weight, time_weight), "low")

    start = l_idx * per_core
    outgoing = lax.dynamic_slice_in_dim(
        latent_map.reshape(tiles, per_tile, row_local, col_local, width), start, per_core, 1
    )
    arrived = lax.all_to_all(outgoing, "tile", split_axis=0, concat_axis=0, tiled=True)
    arrived = arrived.transpose(1, 0, 2, 3, 4).reshape(per_core, tiles * row_local, col_local, width)
    inner_own = lax.dynamic_slice_in_dim(inner_map, start, per_core, 0)
    joined = (arrived.astype(jnp.float32) + inner_own.astype(jnp.float32)).astype(jnp.bfloat16)
    if lax.axis_size("chan") == 2:
        partner = swap(joined, "chan")
        whole = lax.dynamic_slice_in_dim(
            jnp.concatenate([joined, partner, joined], axis=2), c_idx * col_local, 2 * col_local, 2
        )
    else:
        whole = lax.all_gather(joined, "chan", axis=2, tiled=True)

    picks = t_idx * per_tile + start + jnp.arange(per_core)
    chosen = jnp.arange(samples)[None, :] == picks[:, None]
    stamps = jnp.sum(jnp.where(chosen, timestep[None, :], 0), axis=1)
    embedded = time_embedding(stamps)
    mod_own = jnp.dot(embedded, time_weight.astype(jnp.float32), precision=lax.Precision.HIGHEST)
    mod_other = jnp.dot(embedded, time_other.astype(jnp.float32), precision=lax.Precision.HIGHEST)

    def features_of(weight, modulation):
        convolved = convolve(whole, weight)
        return jax.nn.silu(convolved * (1.0 + modulation[:, None, None, :])).astype(jnp.bfloat16)

    feat_own = features_of(conv_weight, mod_own)
    feat_other = features_of(conv_other, mod_other)
    part_own, part_other = swap((feat_own, feat_other), "low")
    first = l_idx == 0
    half_a = jnp.where(first, jnp.concatenate([feat_own, part_other], 0), jnp.concatenate([part_other, feat_own], 0))
    half_b = jnp.where(first, jnp.concatenate([feat_other, part_own], 0), jnp.concatenate([part_own, feat_other], 0))

    rows_total, cols_total = half_a.shape[1], half_a.shape[2]
    tokens = rows_total * cols_total
    weight_a = lax.dynamic_slice_in_dim(attend_weight, l_idx * half, half, 1)
    weight_b = lax.dynamic_slice_in_dim(attend_weight, (1 - l_idx) * half, half, 1)

    def project(part_a, part_b, which):
        return (
            jnp.dot(part_a, weight_a[which], preferred_element_type=jnp.float32)
            + jnp.dot(part_b, weight_b[which], preferred_element_type=jnp.float32)
        ).astype(jnp.bfloat16)

    col_start = c_idx * col_local
    own_a = lax.dynamic_slice_in_dim(half_a, col_start, col_local, 2)
    own_b = lax.dynamic_slice_in_dim(half_b, col_start, col_local, 2)
    queries = project(own_a.reshape(per_tile, -1, half), own_b.reshape(per_tile, -1, half), 0)
    keys = project(half_a.reshape(per_tile, tokens, half), half_b.reshape(per_tile, tokens, half), 1)
    values = project(half_a.reshape(per_tile, tokens, half), half_b.reshape(per_tile, tokens, half), 2)

    def by_head(x):
        n, k, _ = x.shape
        return x.reshape(n, k, heads_local, HEAD).transpose(0, 2, 1, 3).reshape(n * heads_local, k, HEAD)

    q_heads, k_heads, v_heads = by_head(queries), by_head(keys), by_head(values)
    if tokens * tokens * 4 * q_heads.shape[0] <= (8 << 20):
        out = attend(q_heads, k_heads, v_heads)
    else:
        out = lax.map(lambda trio: attend(*(x[None] for x in trio))[0], (q_heads, k_heads, v_heads))
    out = out.reshape(per_tile, heads_local, row_local * tiles, col_local, HEAD)
    return out.transpose(0, 2, 3, 1, 4).reshape(per_tile, row_local * tiles, col_local, heads_local * HEAD)


def solution(mesh):
    in_specs = (
        P("groups", "tile", "chan", None),
        P(("groups", "tile"), None, "chan", None),
        P("groups"),
        P(None, None, None, "low"),
        P(None, "low"),
        P(None, None, "low"),
    )
    out_specs = P(("groups", "tile"), None, "chan", "low")
    return jax.shard_map(
        per_device, mesh=mesh, in_specs=in_specs, out_specs=out_specs, check_vma=False
    )
```

```python
import math

import jax
import jax.numpy as jnp
from jax import lax
from jax.sharding import PartitionSpec as P

HEAD = 64
TE = 256


def time_embedding(timestep):
    halfway = TE // 2
    ladder = jnp.arange(halfway, dtype=jnp.float32)
    frequency = jnp.exp(ladder * (-math.log(10000.0) / halfway))
    angles = timestep.astype(jnp.float32)[:, None] * frequency[None, :]
    return jnp.concatenate([jnp.sin(angles), jnp.cos(angles)], axis=1)


def swap(tree, axis):
    return lax.ppermute(tree, axis, [(0, 1), (1, 0)])


def convolve(joined, weight):
    return lax.conv_general_dilated(
        joined,
        weight,
        window_strides=(1, 1),
        padding=((1, 1), (1, 1)),
        dimension_numbers=("NHWC", "HWIO", "NHWC"),
        preferred_element_type=jnp.float32,
    )


def attend(queries, keys, values):
    scores = jnp.einsum("nqd,nkd->nqk", queries, keys, preferred_element_type=jnp.float32)
    scores = scores * HEAD ** (-0.5)
    row_peak = jnp.max(scores, axis=2, keepdims=True)
    weights = jnp.exp(scores - row_peak)
    totals = jnp.sum(weights, axis=2, keepdims=True)
    summed = jnp.einsum(
        "nqk,nkd->nqd", weights.astype(jnp.bfloat16), values, preferred_element_type=jnp.float32
    )
    return (summed / totals).astype(jnp.bfloat16)


def per_device(latent_map, inner_map, timestep, conv_weight, time_weight, attend_weight):
    tiles = lax.axis_size("tile")
    lows = lax.axis_size("low")
    t_idx = lax.axis_index("tile")
    c_idx = lax.axis_index("chan")
    l_idx = lax.axis_index("low")
    samples, row_local, col_local, width = latent_map.shape
    per_tile = samples // tiles
    per_core = per_tile // lows
    half = conv_weight.shape[3]
    heads_local = attend_weight.shape[2] // HEAD

    conv_other, time_other = swap((conv_weight, time_weight), "low")

    start = l_idx * per_core
    outgoing = lax.dynamic_slice_in_dim(
        latent_map.reshape(tiles, per_tile, row_local, col_local, width), start, per_core, 1
    ).reshape(tiles * per_core, row_local, col_local, width)
    arrived = lax.all_to_all(outgoing, "tile", split_axis=0, concat_axis=1, tiled=True)
    inner_own = lax.dynamic_slice_in_dim(inner_map, start, per_core, 0)
    joined = (arrived.astype(jnp.float32) + inner_own.astype(jnp.float32)).astype(jnp.bfloat16)
    whole = lax.all_gather(joined, "chan", axis=2, tiled=True)

    stamps = lax.dynamic_slice_in_dim(timestep, t_idx * per_tile + start, per_core, 0)
    embedded = time_embedding(stamps)
    mod_own = jnp.dot(embedded, time_weight.astype(jnp.float32), precision=lax.Precision.HIGHEST)
    mod_other = jnp.dot(embedded, time_other.astype(jnp.float32), precision=lax.Precision.HIGHEST)

    def features_of(weight, modulation):
        convolved = convolve(whole, weight)
        return jax.nn.silu(convolved * (1.0 + modulation[:, None, None, :])).astype(jnp.bfloat16)

    feat_own = features_of(conv_weight, mod_own)
    feat_other = features_of(conv_other, mod_other)
    nat_own = lax.dynamic_slice_in_dim(
        jnp.concatenate([feat_own, feat_other, feat_own], axis=3), l_idx * half, 2 * half, 3
    )
    nat_part = swap(nat_own, "low")
    features = lax.dynamic_slice_in_dim(
        jnp.concatenate([nat_own, nat_part, nat_own], axis=0), l_idx * per_core, per_tile, 0
    )
    rows_total, cols_total = features.shape[1], features.shape[2]
    tokens = rows_total * cols_total

    def project(part, which):
        return jnp.dot(part, attend_weight[which], preferred_element_type=jnp.float32).astype(jnp.bfloat16)

    own_cols = lax.dynamic_slice_in_dim(features, c_idx * col_local, col_local, 2)
    flat = features.reshape(per_tile, tokens, width)
    queries = project(own_cols.reshape(per_tile, -1, width), 0)
    keys = project(flat, 1)
    values = project(flat, 2)
    query_count = queries.shape[1]
    if tokens * query_count * 4 * per_tile * heads_local <= (8 << 20):
        split = lambda x: x.reshape(per_tile, x.shape[1], heads_local, HEAD)
        q4, k4, v4 = split(queries), split(keys), split(values)
        scores = jnp.einsum("bqhd,bkhd->bhqk", q4, k4, preferred_element_type=jnp.float32)
        scores = scores * HEAD ** (-0.5)
        row_peak = jnp.max(scores, axis=3, keepdims=True)
        weights = jnp.exp(scores - row_peak)
        totals = jnp.sum(weights, axis=3)
        summed = jnp.einsum(
            "bhqk,bkhd->bqhd", weights.astype(jnp.bfloat16), v4, preferred_element_type=jnp.float32
        )
        out = (summed / totals.transpose(0, 2, 1)[..., None]).astype(jnp.bfloat16)
        return out.reshape(per_tile, rows_total, col_local, heads_local * HEAD)

    def by_head(x):
        n, k, _ = x.shape
        return x.reshape(n, k, heads_local, HEAD).transpose(0, 2, 1, 3).reshape(n * heads_local, k, HEAD)

    q_heads, k_heads, v_heads = by_head(queries), by_head(keys), by_head(values)
    out = lax.map(lambda trio: attend(*(x[None] for x in trio))[0], (q_heads, k_heads, v_heads))
    out = out.reshape(per_tile, heads_local, rows_total, col_local, HEAD)
    return out.transpose(0, 2, 3, 1, 4).reshape(per_tile, rows_total, col_local, heads_local * HEAD)


def solution(mesh):
    in_specs = (
        P("groups", "tile", "chan", None),
        P(("groups", "tile"), None, "chan", None),
        P("groups"),
        P(None, None, None, "low"),
        P(None, "low"),
        P(None, None, "low"),
    )
    out_specs = P(("groups", "tile"), None, "chan", "low")
    return jax.shard_map(
        per_device, mesh=mesh, in_specs=in_specs, out_specs=out_specs, check_vma=False
    )
```

```python
import math

import jax
import jax.numpy as jnp
from jax import lax
from jax.sharding import PartitionSpec as P

HEAD = 64
TE = 256


def time_embedding(timestep):
    halfway = TE // 2
    ladder = jnp.arange(halfway, dtype=jnp.float32)
    frequency = jnp.exp(ladder * (-math.log(10000.0) / halfway))
    angles = timestep.astype(jnp.float32)[:, None] * frequency[None, :]
    return jnp.concatenate([jnp.sin(angles), jnp.cos(angles)], axis=1)


def swap(tree, axis):
    return lax.ppermute(tree, axis, [(0, 1), (1, 0)])


def convolve(joined, weight):
    return lax.conv_general_dilated(
        joined,
        weight,
        window_strides=(1, 1),
        padding=((1, 1), (1, 1)),
        dimension_numbers=("NHWC", "HWIO", "NHWC"),
        preferred_element_type=jnp.float32,
    )


def attend(queries, keys, values):
    scores = jnp.einsum("nqd,nkd->nqk", queries, keys, preferred_element_type=jnp.float32)
    scores = scores * HEAD ** (-0.5)
    row_peak = jnp.max(scores, axis=2, keepdims=True)
    weights = jnp.exp(scores - row_peak)
    totals = jnp.sum(weights, axis=2, keepdims=True)
    summed = jnp.einsum(
        "nqk,nkd->nqd", weights.astype(jnp.bfloat16), values, preferred_element_type=jnp.float32
    )
    return (summed / totals).astype(jnp.bfloat16)


def per_device(latent_map, inner_map, timestep, conv_weight, time_weight, attend_weight):
    tiles = lax.axis_size("tile")
    lows = lax.axis_size("low")
    t_idx = lax.axis_index("tile")
    c_idx = lax.axis_index("chan")
    l_idx = lax.axis_index("low")
    samples, row_local, col_local, width = latent_map.shape
    per_tile = samples // tiles
    per_core = per_tile // lows
    half = conv_weight.shape[3]
    heads_local = attend_weight.shape[2] // HEAD

    conv_other, time_other = swap((conv_weight, time_weight), "low")

    start = l_idx * per_core
    outgoing = lax.dynamic_slice_in_dim(
        latent_map.reshape(tiles, per_tile, row_local, col_local, width), start, per_core, 1
    ).reshape(tiles * per_core, row_local, col_local, width)
    arrived = lax.all_to_all(outgoing, "tile", split_axis=0, concat_axis=1, tiled=True)
    inner_own = lax.dynamic_slice_in_dim(inner_map, start, per_core, 0)
    joined = (arrived.astype(jnp.float32) + inner_own.astype(jnp.float32)).astype(jnp.bfloat16)
    whole = lax.all_gather(joined, "chan", axis=2, tiled=True)

    stamps = lax.dynamic_slice_in_dim(timestep, t_idx * per_tile + start, per_core, 0)
    embedded = time_embedding(stamps)
    mod_own = jnp.dot(embedded, time_weight.astype(jnp.float32), precision=lax.Precision.HIGHEST)
    mod_other = jnp.dot(embedded, time_other.astype(jnp.float32), precision=lax.Precision.HIGHEST)

    def features_of(weight, modulation):
        convolved = convolve(whole, weight)
        return jax.nn.silu(convolved * (1.0 + modulation[:, None, None, :])).astype(jnp.bfloat16)

    feat_own = features_of(conv_weight, mod_own)
    feat_other = features_of(conv_other, mod_other)
    nat_own = lax.dynamic_slice_in_dim(
        jnp.concatenate([feat_own, feat_other, feat_own], axis=3), l_idx * half, 2 * half, 3
    )
    nat_part = swap(nat_own, "low")
    features = lax.dynamic_slice_in_dim(
        jnp.concatenate([nat_own, nat_part, nat_own], axis=0), l_idx * per_core, per_tile, 0
    )
    rows_total, cols_total = features.shape[1], features.shape[2]
    tokens = rows_total * cols_total

    def project(part, which):
        return jnp.dot(part, attend_weight[which], preferred_element_type=jnp.float32).astype(jnp.bfloat16)

    own_cols = lax.dynamic_slice_in_dim(features, c_idx * col_local, col_local, 2)
    flat = features.reshape(per_tile, tokens, width)
    queries = project(own_cols.reshape(per_tile, -1, width), 0)
    keys = project(flat, 1)
    values = project(flat, 2)
    query_count = queries.shape[1]
    if tokens * query_count * 4 * per_tile * heads_local <= (8 << 20):
        lanes = heads_local * HEAD
        row_head = jnp.arange(heads_local * tokens)[:, None] // tokens
        lane_head = jnp.arange(lanes)[None, :] // HEAD
        own_head = row_head == lane_head
        key_blocks = jnp.where(own_head, jnp.tile(keys, (1, heads_local, 1)), 0)
        value_blocks = jnp.where(own_head, jnp.tile(values, (1, heads_local, 1)), 0)
        scores = jnp.einsum("bqc,bjc->bqj", queries, key_blocks, preferred_element_type=jnp.float32)
        scores = (scores * HEAD ** (-0.5)).reshape(per_tile, query_count, heads_local, tokens)
        row_peak = jnp.max(scores, axis=3, keepdims=True)
        weights = jnp.exp(scores - row_peak)
        totals = jnp.sum(weights, axis=3)
        rounded = weights.astype(jnp.bfloat16).reshape(per_tile, query_count, heads_local * tokens)
        summed = jnp.einsum("bqj,bjc->bqc", rounded, value_blocks, preferred_element_type=jnp.float32)
        out = (summed / jnp.repeat(totals, HEAD, axis=2)).astype(jnp.bfloat16)
        return out.reshape(per_tile, rows_total, col_local, lanes)

    def by_head(x):
        n, k, _ = x.shape
        return x.reshape(n, k, heads_local, HEAD).transpose(0, 2, 1, 3).reshape(n * heads_local, k, HEAD)

    q_heads, k_heads, v_heads = by_head(queries), by_head(keys), by_head(values)
    out = lax.map(lambda trio: attend(*(x[None] for x in trio))[0], (q_heads, k_heads, v_heads))
    out = out.reshape(per_tile, heads_local, rows_total, col_local, HEAD)
    return out.transpose(0, 2, 3, 1, 4).reshape(per_tile, rows_total, col_local, heads_local * HEAD)


def solution(mesh):
    in_specs = (
        P("groups", "tile", "chan", None),
        P(("groups", "tile"), None, "chan", None),
        P("groups"),
        P(None, None, None, "low"),
        P(None, "low"),
        P(None, None, "low"),
    )
    out_specs = P(("groups", "tile"), None, "chan", "low")
    return jax.shard_map(
        per_device, mesh=mesh, in_specs=in_specs, out_specs=out_specs, check_vma=False
    )
```

```python
import math

import jax
import jax.numpy as jnp
from jax import lax
from jax.sharding import PartitionSpec as P

HEAD = 64
TE = 256


def time_embedding(timestep):
    halfway = TE // 2
    ladder = jnp.arange(halfway, dtype=jnp.float32)
    frequency = jnp.exp(ladder * (-math.log(10000.0) / halfway))
    angles = timestep.astype(jnp.float32)[:, None] * frequency[None, :]
    return jnp.concatenate([jnp.sin(angles), jnp.cos(angles)], axis=1)


def swap(tree, axis):
    return lax.ppermute(tree, axis, [(0, 1), (1, 0)])


def convolve(joined, weight):
    return lax.conv_general_dilated(
        joined,
        weight,
        window_strides=(1, 1),
        padding=((1, 1), (1, 1)),
        dimension_numbers=("NHWC", "HWIO", "NHWC"),
        preferred_element_type=jnp.float32,
    )


def attend(queries, keys, values):
    scores = jnp.einsum("nqd,nkd->nqk", queries, keys, preferred_element_type=jnp.float32)
    scores = scores * HEAD ** (-0.5)
    row_peak = jnp.max(scores, axis=2, keepdims=True)
    weights = jnp.exp(scores - row_peak)
    totals = jnp.sum(weights, axis=2, keepdims=True)
    summed = jnp.einsum(
        "nqk,nkd->nqd", weights.astype(jnp.bfloat16), values, preferred_element_type=jnp.float32
    )
    return (summed / totals).astype(jnp.bfloat16)


def per_device(latent_map, inner_map, timestep, conv_weight, time_weight, attend_weight):
    tiles = lax.axis_size("tile")
    lows = lax.axis_size("low")
    t_idx = lax.axis_index("tile")
    c_idx = lax.axis_index("chan")
    l_idx = lax.axis_index("low")
    samples, row_local, col_local, width = latent_map.shape
    per_tile = samples // tiles
    per_core = per_tile // lows
    half = conv_weight.shape[3]
    heads_local = attend_weight.shape[2] // HEAD

    conv_other, time_other = swap((conv_weight, time_weight), "low")

    start = l_idx * per_core
    chans = lax.axis_size("chan")
    blocks = lax.dynamic_slice_in_dim(
        latent_map.reshape(tiles, per_tile, row_local, col_local, width), start, per_core, 1
    )
    inner_own = lax.dynamic_slice_in_dim(inner_map, start, per_core, 0)
    if tiles * chans <= 8 and chans == 2:
        outgoing = jnp.broadcast_to(blocks[:, None], (tiles, chans) + blocks.shape[1:])
        arrived = lax.all_to_all(
            outgoing.reshape((tiles * chans,) + blocks.shape[1:]), ("tile", "chan"), 0, 0, tiled=True
        )
        arrived = arrived.reshape(tiles, chans, per_core, row_local, col_local, width)
        latent_whole = arrived.transpose(2, 0, 3, 1, 4, 5).reshape(
            per_core, tiles * row_local, chans * col_local, width
        )
        partner = swap(inner_own, "chan")
        inner_whole = lax.dynamic_slice_in_dim(
            jnp.concatenate([inner_own, partner, inner_own], axis=2), c_idx * col_local, 2 * col_local, 2
        )
        whole = (latent_whole.astype(jnp.float32) + inner_whole.astype(jnp.float32)).astype(jnp.bfloat16)
    else:
        outgoing = blocks.reshape(tiles * per_core, row_local, col_local, width)
        arrived = lax.all_to_all(outgoing, "tile", split_axis=0, concat_axis=1, tiled=True)
        joined = (arrived.astype(jnp.float32) + inner_own.astype(jnp.float32)).astype(jnp.bfloat16)
        whole = lax.all_gather(joined, "chan", axis=2, tiled=True)

    stamps = lax.dynamic_slice_in_dim(timestep, t_idx * per_tile + start, per_core, 0)
    embedded = time_embedding(stamps)
    mod_own = jnp.dot(embedded, time_weight.astype(jnp.float32), precision=lax.Precision.HIGHEST)
    mod_other = jnp.dot(embedded, time_other.astype(jnp.float32), precision=lax.Precision.HIGHEST)

    def features_of(weight, modulation):
        convolved = convolve(whole, weight)
        return jax.nn.silu(convolved * (1.0 + modulation[:, None, None, :])).astype(jnp.bfloat16)

    feat_own = features_of(conv_weight, mod_own)
    feat_other = features_of(conv_other, mod_other)
    nat_own = lax.dynamic_slice_in_dim(
        jnp.concatenate([feat_own, feat_other, feat_own], axis=3), l_idx * half, 2 * half, 3
    )
    nat_part = swap(nat_own, "low")
    features = lax.dynamic_slice_in_dim(
        jnp.concatenate([nat_own, nat_part, nat_own], axis=0), l_idx * per_core, per_tile, 0
    )
    rows_total, cols_total = features.shape[1], features.shape[2]
    tokens = rows_total * cols_total

    def project(part, which):
        return jnp.dot(part, attend_weight[which], preferred_element_type=jnp.float32).astype(jnp.bfloat16)

    own_cols = lax.dynamic_slice_in_dim(features, c_idx * col_local, col_local, 2)
    flat = features.reshape(per_tile, tokens, width)
    queries = project(own_cols.reshape(per_tile, -1, width), 0)
    keys = project(flat, 1)
    values = project(flat, 2)
    query_count = queries.shape[1]
    if tokens * query_count * 4 * per_tile * heads_local <= (8 << 20):
        split = lambda x: x.reshape(per_tile, x.shape[1], heads_local, HEAD)
        q4, k4, v4 = split(queries), split(keys), split(values)
        scores = jnp.einsum("bqhd,bkhd->bhqk", q4, k4, preferred_element_type=jnp.float32)
        scores = scores * HEAD ** (-0.5)
        row_peak = jnp.max(scores, axis=3, keepdims=True)
        weights = jnp.exp(scores - row_peak)
        totals = jnp.sum(weights, axis=3)
        summed = jnp.einsum(
            "bhqk,bkhd->bqhd", weights.astype(jnp.bfloat16), v4, preferred_element_type=jnp.float32
        )
        out = (summed / totals.transpose(0, 2, 1)[..., None]).astype(jnp.bfloat16)
        return out.reshape(per_tile, rows_total, col_local, heads_local * HEAD)

    def by_head(x):
        n, k, _ = x.shape
        return x.reshape(n, k, heads_local, HEAD).transpose(0, 2, 1, 3).reshape(n * heads_local, k, HEAD)

    q_heads, k_heads, v_heads = by_head(queries), by_head(keys), by_head(values)
    out = lax.map(lambda trio: attend(*(x[None] for x in trio))[0], (q_heads, k_heads, v_heads))
    out = out.reshape(per_tile, heads_local, rows_total, col_local, HEAD)
    return out.transpose(0, 2, 3, 1, 4).reshape(per_tile, rows_total, col_local, heads_local * HEAD)


def solution(mesh):
    in_specs = (
        P("groups", "tile", "chan", None),
        P(("groups", "tile"), None, "chan", None),
        P("groups"),
        P(None, None, None, "low"),
        P(None, "low"),
        P(None, None, "low"),
    )
    out_specs = P(("groups", "tile"), None, "chan", "low")
    return jax.shard_map(
        per_device, mesh=mesh, in_specs=in_specs, out_specs=out_specs, check_vma=False
    )
```

```python
import math

import jax
import jax.numpy as jnp
from jax import lax
from jax.sharding import PartitionSpec as P

HEAD = 64
TE = 256


def time_embedding(timestep):
    halfway = TE // 2
    ladder = jnp.arange(halfway, dtype=jnp.float32)
    frequency = jnp.exp(ladder * (-math.log(10000.0) / halfway))
    angles = timestep.astype(jnp.float32)[:, None] * frequency[None, :]
    return jnp.concatenate([jnp.sin(angles), jnp.cos(angles)], axis=1)


def swap(tree, axis):
    return lax.ppermute(tree, axis, [(0, 1), (1, 0)])


def convolve(joined, weight):
    return lax.conv_general_dilated(
        joined,
        weight,
        window_strides=(1, 1),
        padding=((1, 1), (1, 1)),
        dimension_numbers=("NHWC", "HWIO", "NHWC"),
        preferred_element_type=jnp.float32,
    )


def attend(queries, keys, values):
    scores = jnp.einsum("nqd,nkd->nqk", queries, keys, preferred_element_type=jnp.float32)
    scores = scores * HEAD ** (-0.5)
    row_peak = jnp.max(scores, axis=2, keepdims=True)
    weights = jnp.exp(scores - row_peak)
    totals = jnp.sum(weights, axis=2, keepdims=True)
    summed = jnp.einsum(
        "nqk,nkd->nqd", weights.astype(jnp.bfloat16), values, preferred_element_type=jnp.float32
    )
    return (summed / totals).astype(jnp.bfloat16)


def per_device(latent_map, inner_map, timestep, conv_weight, time_weight, attend_weight):
    tiles = lax.axis_size("tile")
    lows = lax.axis_size("low")
    t_idx = lax.axis_index("tile")
    c_idx = lax.axis_index("chan")
    l_idx = lax.axis_index("low")
    samples, row_local, col_local, width = latent_map.shape
    per_tile = samples // tiles
    per_core = per_tile // lows
    half = conv_weight.shape[3]
    heads_local = attend_weight.shape[2] // HEAD

    conv_other, time_other = swap((conv_weight, time_weight), "low")

    start = l_idx * per_core
    outgoing = lax.dynamic_slice_in_dim(
        latent_map.reshape(tiles, per_tile, row_local, col_local, width), start, per_core, 1
    ).reshape(tiles * per_core, row_local, col_local, width)
    arrived = lax.all_to_all(outgoing, "tile", split_axis=0, concat_axis=1, tiled=True)
    inner_own = lax.dynamic_slice_in_dim(inner_map, start, per_core, 0)
    joined = (arrived.astype(jnp.float32) + inner_own.astype(jnp.float32)).astype(jnp.bfloat16)
    whole = lax.all_gather(joined, "chan", axis=2, tiled=True)

    stamps = lax.dynamic_slice_in_dim(timestep, t_idx * per_tile + start, per_core, 0)
    embedded = time_embedding(stamps)
    mod_own = jnp.dot(embedded, time_weight.astype(jnp.float32), precision=lax.Precision.HIGHEST)
    mod_other = jnp.dot(embedded, time_other.astype(jnp.float32), precision=lax.Precision.HIGHEST)

    def features_of(weight, modulation):
        convolved = convolve(whole, weight)
        return jax.nn.silu(convolved * (1.0 + modulation[:, None, None, :])).astype(jnp.bfloat16)

    feat_own = features_of(conv_weight, mod_own)
    feat_other = features_of(conv_other, mod_other)
    nat_own = lax.dynamic_slice_in_dim(
        jnp.concatenate([feat_own, feat_other, feat_own], axis=3), l_idx * half, 2 * half, 3
    )
    nat_part = swap(nat_own, "low")
    features = lax.dynamic_slice_in_dim(
        jnp.concatenate([nat_own, nat_part, nat_own], axis=0), l_idx * per_core, per_tile, 0
    )
    rows_total, cols_total = features.shape[1], features.shape[2]
    tokens = rows_total * cols_total

    def project(part, which):
        return jnp.dot(part, attend_weight[which], preferred_element_type=jnp.float32).astype(jnp.bfloat16)

    own_cols = lax.dynamic_slice_in_dim(features, c_idx * col_local, col_local, 2)
    flat = features.reshape(per_tile, tokens, width)
    queries = project(own_cols.reshape(per_tile, -1, width), 0)
    keys = project(flat, 1)
    values = project(flat, 2)
    query_count = queries.shape[1]
    if tokens * query_count * 4 * per_tile * heads_local <= (8 << 20):
        split = lambda x: x.reshape(per_tile, x.shape[1], heads_local, HEAD)
        q4, k4, v4 = split(queries), split(keys), split(values)
        scores = jnp.einsum("bqhd,bkhd->bhqk", q4, k4, preferred_element_type=jnp.float32)
        scores = scores * HEAD ** (-0.5)
        row_peak = jnp.max(scores, axis=3, keepdims=True)
        weights = jnp.exp(scores - row_peak)
        totals = jnp.sum(weights, axis=3)
        summed = jnp.einsum(
            "bhqk,bkc->bhqc", weights.astype(jnp.bfloat16), values, preferred_element_type=jnp.float32
        )
        lane_head = jnp.arange(heads_local * HEAD)[None, :] // HEAD == jnp.arange(heads_local)[:, None]
        scaled = summed / totals[..., None]
        out = jnp.sum(jnp.where(lane_head[None, :, None, :], scaled, 0.0), axis=1).astype(jnp.bfloat16)
        return out.reshape(per_tile, rows_total, col_local, heads_local * HEAD)

    def by_head(x):
        n, k, _ = x.shape
        return x.reshape(n, k, heads_local, HEAD).transpose(0, 2, 1, 3).reshape(n * heads_local, k, HEAD)

    q_heads, k_heads, v_heads = by_head(queries), by_head(keys), by_head(values)
    out = lax.map(lambda trio: attend(*(x[None] for x in trio))[0], (q_heads, k_heads, v_heads))
    out = out.reshape(per_tile, heads_local, rows_total, col_local, HEAD)
    return out.transpose(0, 2, 3, 1, 4).reshape(per_tile, rows_total, col_local, heads_local * HEAD)


def solution(mesh):
    in_specs = (
        P("groups", "tile", "chan", None),
        P(("groups", "tile"), None, "chan", None),
        P("groups"),
        P(None, None, None, "low"),
        P(None, "low"),
        P(None, None, "low"),
    )
    out_specs = P(("groups", "tile"), None, "chan", "low")
    return jax.shard_map(
        per_device, mesh=mesh, in_specs=in_specs, out_specs=out_specs, check_vma=False
    )
```

```python
import math

import jax
import jax.numpy as jnp
from jax import lax
from jax.sharding import PartitionSpec as P

HEAD = 64
TE = 256


def time_embedding(timestep):
    halfway = TE // 2
    ladder = jnp.arange(halfway, dtype=jnp.float32)
    frequency = jnp.exp(ladder * (-math.log(10000.0) / halfway))
    angles = timestep.astype(jnp.float32)[:, None] * frequency[None, :]
    return jnp.concatenate([jnp.sin(angles), jnp.cos(angles)], axis=1)


def swap(tree, axis):
    return lax.ppermute(tree, axis, [(0, 1), (1, 0)])


def convolve(joined, weight):
    return lax.conv_general_dilated(
        joined,
        weight,
        window_strides=(1, 1),
        padding=((1, 1), (1, 1)),
        dimension_numbers=("NHWC", "HWIO", "NHWC"),
        preferred_element_type=jnp.float32,
    )


def attend(queries, keys, values):
    scores = jnp.einsum("nqd,nkd->nqk", queries, keys, preferred_element_type=jnp.float32)
    scores = scores * HEAD ** (-0.5)
    row_peak = jnp.max(scores, axis=2, keepdims=True)
    weights = jnp.exp(scores - row_peak)
    totals = jnp.sum(weights, axis=2, keepdims=True)
    summed = jnp.einsum(
        "nqk,nkd->nqd", weights.astype(jnp.bfloat16), values, preferred_element_type=jnp.float32
    )
    return (summed / totals).astype(jnp.bfloat16)


def per_device(latent_map, inner_map, timestep, conv_weight, time_weight, attend_weight):
    tiles = lax.axis_size("tile")
    lows = lax.axis_size("low")
    t_idx = lax.axis_index("tile")
    c_idx = lax.axis_index("chan")
    l_idx = lax.axis_index("low")
    samples, row_local, col_local, width = latent_map.shape
    per_tile = samples // tiles
    per_core = per_tile // lows
    half = conv_weight.shape[3]
    heads_local = attend_weight.shape[2] // HEAD

    conv_other, time_other = swap((conv_weight, time_weight), "low")

    start = l_idx * per_core
    outgoing = lax.dynamic_slice_in_dim(
        latent_map.reshape(tiles, per_tile, row_local * col_local, width), start, per_core, 1
    ).reshape(tiles * per_core, row_local * col_local, width)
    arrived = lax.all_to_all(outgoing, "tile", split_axis=0, concat_axis=0, tiled=True)
    arrived = arrived.reshape(tiles, per_core, row_local, col_local, width).transpose(1, 0, 2, 3, 4)
    arrived = arrived.reshape(per_core, tiles * row_local, col_local, width)
    inner_own = lax.dynamic_slice_in_dim(inner_map, start, per_core, 0)
    joined = (arrived.astype(jnp.float32) + inner_own.astype(jnp.float32)).astype(jnp.bfloat16)
    whole = lax.all_gather(joined, "chan", axis=2, tiled=True)

    stamps = lax.dynamic_slice_in_dim(timestep, t_idx * per_tile + start, per_core, 0)
    embedded = time_embedding(stamps)
    mod_own = jnp.dot(embedded, time_weight.astype(jnp.float32), precision=lax.Precision.HIGHEST)
    mod_other = jnp.dot(embedded, time_other.astype(jnp.float32), precision=lax.Precision.HIGHEST)

    def features_of(weight, modulation):
        convolved = convolve(whole, weight)
        return jax.nn.silu(convolved * (1.0 + modulation[:, None, None, :])).astype(jnp.bfloat16)

    feat_own = features_of(conv_weight, mod_own)
    feat_other = features_of(conv_other, mod_other)
    nat_own = lax.dynamic_slice_in_dim(
        jnp.concatenate([feat_own, feat_other, feat_own], axis=3), l_idx * half, 2 * half, 3
    )
    nat_part = swap(nat_own, "low")
    features = lax.dynamic_slice_in_dim(
        jnp.concatenate([nat_own, nat_part, nat_own], axis=0), l_idx * per_core, per_tile, 0
    )
    rows_total, cols_total = features.shape[1], features.shape[2]
    tokens = rows_total * cols_total

    def project(part, which):
        return jnp.dot(part, attend_weight[which], preferred_element_type=jnp.float32).astype(jnp.bfloat16)

    own_cols = lax.dynamic_slice_in_dim(features, c_idx * col_local, col_local, 2)
    flat = features.reshape(per_tile, tokens, width)
    queries = project(own_cols.reshape(per_tile, -1, width), 0)
    keys = project(flat, 1)
    values = project(flat, 2)
    query_count = queries.shape[1]
    if tokens * query_count * 4 * per_tile * heads_local <= (8 << 20):
        split = lambda x: x.reshape(per_tile, x.shape[1], heads_local, HEAD)
        q4, k4, v4 = split(queries), split(keys), split(values)
        scores = jnp.einsum("bqhd,bkhd->bhqk", q4, k4, preferred_element_type=jnp.float32)
        scores = scores * HEAD ** (-0.5)
        row_peak = jnp.max(scores, axis=3, keepdims=True)
        weights = jnp.exp(scores - row_peak)
        totals = jnp.sum(weights, axis=3)
        summed = jnp.einsum(
            "bhqk,bkhd->bqhd", weights.astype(jnp.bfloat16), v4, preferred_element_type=jnp.float32
        )
        out = (summed / totals.transpose(0, 2, 1)[..., None]).astype(jnp.bfloat16)
        return out.reshape(per_tile, rows_total, col_local, heads_local * HEAD)

    def by_head(x):
        n, k, _ = x.shape
        return x.reshape(n, k, heads_local, HEAD).transpose(0, 2, 1, 3).reshape(n * heads_local, k, HEAD)

    q_heads, k_heads, v_heads = by_head(queries), by_head(keys), by_head(values)
    out = lax.map(lambda trio: attend(*(x[None] for x in trio))[0], (q_heads, k_heads, v_heads))
    out = out.reshape(per_tile, heads_local, rows_total, col_local, HEAD)
    return out.transpose(0, 2, 3, 1, 4).reshape(per_tile, rows_total, col_local, heads_local * HEAD)


def solution(mesh):
    in_specs = (
        P("groups", "tile", "chan", None),
        P(("groups", "tile"), None, "chan", None),
        P("groups"),
        P(None, None, None, "low"),
        P(None, "low"),
        P(None, None, "low"),
    )
    out_specs = P(("groups", "tile"), None, "chan", "low")
    return jax.shard_map(
        per_device, mesh=mesh, in_specs=in_specs, out_specs=out_specs, check_vma=False
    )
```

```python
import math

import jax
import jax.numpy as jnp
from jax import lax
from jax.sharding import PartitionSpec as P

HEAD = 64
TE = 256


def time_embedding(timestep):
    halfway = TE // 2
    ladder = jnp.arange(halfway, dtype=jnp.float32)
    frequency = jnp.exp(ladder * (-math.log(10000.0) / halfway))
    angles = timestep.astype(jnp.float32)[:, None] * frequency[None, :]
    return jnp.concatenate([jnp.sin(angles), jnp.cos(angles)], axis=1)


def swap(tree, axis):
    return lax.ppermute(tree, axis, [(0, 1), (1, 0)])


def convolve(joined, weight):
    return lax.conv_general_dilated(
        joined,
        weight,
        window_strides=(1, 1),
        padding=((1, 1), (1, 1)),
        dimension_numbers=("NHWC", "HWIO", "NHWC"),
        preferred_element_type=jnp.float32,
    )


def attend(queries, keys, values):
    scores = jnp.einsum("nqd,nkd->nqk", queries, keys, preferred_element_type=jnp.float32)
    scores = scores * HEAD ** (-0.5)
    row_peak = jnp.max(scores, axis=2, keepdims=True)
    weights = jnp.exp(scores - row_peak)
    totals = jnp.sum(weights, axis=2, keepdims=True)
    summed = jnp.einsum(
        "nqk,nkd->nqd", weights.astype(jnp.bfloat16), values, preferred_element_type=jnp.float32
    )
    return (summed / totals).astype(jnp.bfloat16)


def per_device(latent_map, inner_map, timestep, conv_weight, time_weight, attend_weight):
    tiles = lax.axis_size("tile")
    lows = lax.axis_size("low")
    t_idx = lax.axis_index("tile")
    c_idx = lax.axis_index("chan")
    l_idx = lax.axis_index("low")
    samples, row_local, col_local, width = latent_map.shape
    per_tile = samples // tiles
    per_core = per_tile // lows
    half = conv_weight.shape[3]
    heads_local = attend_weight.shape[2] // HEAD

    conv_other, time_other, attend_other = swap((conv_weight, time_weight, attend_weight), "low")
    attend_full = lax.dynamic_slice_in_dim(
        jnp.concatenate([attend_weight, attend_other, attend_weight], axis=2), l_idx * half, 2 * half, 2
    )

    start = l_idx * per_core
    outgoing = lax.dynamic_slice_in_dim(
        latent_map.reshape(tiles, per_tile, row_local, col_local, width), start, per_core, 1
    ).reshape(tiles * per_core, row_local, col_local, width)
    arrived = lax.all_to_all(outgoing, "tile", split_axis=0, concat_axis=1, tiled=True)
    inner_own = lax.dynamic_slice_in_dim(inner_map, start, per_core, 0)
    joined = (arrived.astype(jnp.float32) + inner_own.astype(jnp.float32)).astype(jnp.bfloat16)
    whole = lax.all_gather(joined, "chan", axis=2, tiled=True)

    stamps = lax.dynamic_slice_in_dim(timestep, t_idx * per_tile + start, per_core, 0)
    embedded = time_embedding(stamps)
    mod_own = jnp.dot(embedded, time_weight.astype(jnp.float32), precision=lax.Precision.HIGHEST)
    mod_other = jnp.dot(embedded, time_other.astype(jnp.float32), precision=lax.Precision.HIGHEST)

    def features_of(weight, modulation):
        convolved = convolve(whole, weight)
        return jax.nn.silu(convolved * (1.0 + modulation[:, None, None, :])).astype(jnp.bfloat16)

    feat_own = features_of(conv_weight, mod_own)
    feat_other = features_of(conv_other, mod_other)
    nat_own = lax.dynamic_slice_in_dim(
        jnp.concatenate([feat_own, feat_other, feat_own], axis=3), l_idx * half, 2 * half, 3
    )
    features = nat_own
    rows_total, cols_total = features.shape[1], features.shape[2]
    tokens = rows_total * cols_total
    heads_all = attend_full.shape[2] // HEAD

    def project(part, which):
        return jnp.dot(part, attend_full[which], preferred_element_type=jnp.float32).astype(jnp.bfloat16)

    own_cols = lax.dynamic_slice_in_dim(features, c_idx * col_local, col_local, 2)
    flat = features.reshape(per_core, tokens, width)
    queries = project(own_cols.reshape(per_core, -1, width), 0)
    keys = project(flat, 1)
    values = project(flat, 2)
    query_count = queries.shape[1]
    if tokens * query_count * 4 * per_core * heads_all <= (8 << 20):
        split = lambda x: x.reshape(per_core, x.shape[1], heads_all, HEAD)
        q4, k4, v4 = split(queries), split(keys), split(values)
        scores = jnp.einsum("bqhd,bkhd->bhqk", q4, k4, preferred_element_type=jnp.float32)
        scores = scores * HEAD ** (-0.5)
        row_peak = jnp.max(scores, axis=3, keepdims=True)
        weights = jnp.exp(scores - row_peak)
        totals = jnp.sum(weights, axis=3)
        summed = jnp.einsum(
            "bhqk,bkhd->bqhd", weights.astype(jnp.bfloat16), v4, preferred_element_type=jnp.float32
        )
        out = (summed / totals.transpose(0, 2, 1)[..., None]).astype(jnp.bfloat16)
    else:
        def by_head(x):
            n, k, _ = x.shape
            return x.reshape(n, k, heads_all, HEAD).transpose(0, 2, 1, 3).reshape(n * heads_all, k, HEAD)

        trio = (by_head(queries), by_head(keys), by_head(values))
        out = lax.map(lambda one: attend(*(x[None] for x in one))[0], trio)
        out = out.reshape(per_core, heads_all, query_count, HEAD).transpose(0, 2, 1, 3)
    out = out.reshape(per_core, rows_total, col_local, heads_all * HEAD)
    kept = lax.dynamic_slice_in_dim(out, l_idx * half, half, 3)
    given = lax.dynamic_slice_in_dim(out, (1 - l_idx) * half, half, 3)
    got = swap(given, "low")
    return lax.dynamic_slice_in_dim(
        jnp.concatenate([kept, got, kept], axis=0), l_idx * per_core, per_tile, 0
    )


def solution(mesh):
    in_specs = (
        P("groups", "tile", "chan", None),
        P(("groups", "tile"), None, "chan", None),
        P("groups"),
        P(None, None, None, "low"),
        P(None, "low"),
        P(None, None, "low"),
    )
    out_specs = P(("groups", "tile"), None, "chan", "low")
    return jax.shard_map(
        per_device, mesh=mesh, in_specs=in_specs, out_specs=out_specs, check_vma=False
    )
```

```python
import math

import jax
import jax.numpy as jnp
from jax import lax
from jax.experimental import pallas as pl
from jax.experimental.pallas import tpu as pltpu
from jax.sharding import PartitionSpec as P

HEAD = 64
TE = 256


def time_embedding(timestep):
    halfway = TE // 2
    ladder = jnp.arange(halfway, dtype=jnp.float32)
    frequency = jnp.exp(ladder * (-math.log(10000.0) / halfway))
    angles = timestep.astype(jnp.float32)[:, None] * frequency[None, :]
    return jnp.concatenate([jnp.sin(angles), jnp.cos(angles)], axis=1)


def swap(tree, axis):
    return lax.ppermute(tree, axis, [(0, 1), (1, 0)])


def convolve(joined, weight):
    return lax.conv_general_dilated(
        joined,
        weight,
        window_strides=(1, 1),
        padding=((1, 1), (1, 1)),
        dimension_numbers=("NHWC", "HWIO", "NHWC"),
        preferred_element_type=jnp.float32,
    )


def attend(queries, keys, values):
    scores = jnp.einsum("nqd,nkd->nqk", queries, keys, preferred_element_type=jnp.float32)
    scores = scores * HEAD ** (-0.5)
    row_peak = jnp.max(scores, axis=2, keepdims=True)
    weights = jnp.exp(scores - row_peak)
    totals = jnp.sum(weights, axis=2, keepdims=True)
    summed = jnp.einsum(
        "nqk,nkd->nqd", weights.astype(jnp.bfloat16), values, preferred_element_type=jnp.float32
    )
    return (summed / totals).astype(jnp.bfloat16)


def attention_kernel(q_ref, k_ref, v_ref, o_ref):
    samples, _, lanes = q_ref.shape
    for sample in range(samples):
        for head in range(lanes // HEAD):
            part = slice(head * HEAD, (head + 1) * HEAD)
            queries = q_ref[sample, :, part]
            keys = k_ref[sample, :, part]
            scores = lax.dot_general(
                queries, keys, (((1,), (1,)), ((), ())), preferred_element_type=jnp.float32
            )
            scores = scores * HEAD ** (-0.5)
            row_peak = jnp.max(scores, axis=1, keepdims=True)
            weights = jnp.exp(scores - row_peak)
            totals = jnp.sum(weights, axis=1, keepdims=True)
            summed = jnp.dot(
                weights.astype(jnp.bfloat16), v_ref[sample, :, part], preferred_element_type=jnp.float32
            )
            o_ref[sample, :, part] = (summed / totals).astype(o_ref.dtype)


def attention_call(queries, keys, values):
    samples, query_count, lanes = queries.shape
    key_count = keys.shape[1]
    flops = 4 * samples * query_count * key_count * lanes
    moved = 2 * (2 * queries.size + keys.size + values.size)
    return pl.pallas_call(
        attention_kernel,
        out_shape=jax.ShapeDtypeStruct(queries.shape, jnp.bfloat16),
        in_specs=[pl.BlockSpec(memory_space=pltpu.VMEM)] * 3,
        out_specs=pl.BlockSpec(memory_space=pltpu.VMEM),
        cost_estimate=pl.CostEstimate(
            flops=flops, transcendentals=samples * query_count * key_count * lanes // HEAD, bytes_accessed=moved
        ),
    )(queries, keys, values)


def per_device(latent_map, inner_map, timestep, conv_weight, time_weight, attend_weight):
    tiles = lax.axis_size("tile")
    lows = lax.axis_size("low")
    t_idx = lax.axis_index("tile")
    c_idx = lax.axis_index("chan")
    l_idx = lax.axis_index("low")
    samples, row_local, col_local, width = latent_map.shape
    per_tile = samples // tiles
    per_core = per_tile // lows
    half = conv_weight.shape[3]
    heads_local = attend_weight.shape[2] // HEAD

    conv_other, time_other = swap((conv_weight, time_weight), "low")

    start = l_idx * per_core
    outgoing = lax.dynamic_slice_in_dim(
        latent_map.reshape(tiles, per_tile, row_local, col_local, width), start, per_core, 1
    ).reshape(tiles * per_core, row_local, col_local, width)
    arrived = lax.all_to_all(outgoing, "tile", split_axis=0, concat_axis=1, tiled=True)
    inner_own = lax.dynamic_slice_in_dim(inner_map, start, per_core, 0)
    joined = (arrived.astype(jnp.float32) + inner_own.astype(jnp.float32)).astype(jnp.bfloat16)
    whole = lax.all_gather(joined, "chan", axis=2, tiled=True)

    stamps = lax.dynamic_slice_in_dim(timestep, t_idx * per_tile + start, per_core, 0)
    embedded = time_embedding(stamps)
    mod_own = jnp.dot(embedded, time_weight.astype(jnp.float32), precision=lax.Precision.HIGHEST)
    mod_other = jnp.dot(embedded, time_other.astype(jnp.float32), precision=lax.Precision.HIGHEST)

    def features_of(weight, modulation):
        convolved = convolve(whole, weight)
        return jax.nn.silu(convolved * (1.0 + modulation[:, None, None, :])).astype(jnp.bfloat16)

    feat_own = features_of(conv_weight, mod_own)
    feat_other = features_of(conv_other, mod_other)
    nat_own = lax.dynamic_slice_in_dim(
        jnp.concatenate([feat_own, feat_other, feat_own], axis=3), l_idx * half, 2 * half, 3
    )
    nat_part = swap(nat_own, "low")
    features = lax.dynamic_slice_in_dim(
        jnp.concatenate([nat_own, nat_part, nat_own], axis=0), l_idx * per_core, per_tile, 0
    )
    rows_total, cols_total = features.shape[1], features.shape[2]
    tokens = rows_total * cols_total

    def project(part, which):
        return jnp.dot(part, attend_weight[which], preferred_element_type=jnp.float32).astype(jnp.bfloat16)

    own_cols = lax.dynamic_slice_in_dim(features, c_idx * col_local, col_local, 2)
    flat = features.reshape(per_tile, tokens, width)
    queries = project(own_cols.reshape(per_tile, -1, width), 0)
    keys = project(flat, 1)
    values = project(flat, 2)
    query_count = queries.shape[1]
    if tokens * query_count * 4 * per_tile * heads_local <= (8 << 20):
        out = attention_call(queries, keys, values)
        return out.reshape(per_tile, rows_total, col_local, heads_local * HEAD)

    def by_head(x):
        n, k, _ = x.shape
        return x.reshape(n, k, heads_local, HEAD).transpose(0, 2, 1, 3).reshape(n * heads_local, k, HEAD)

    q_heads, k_heads, v_heads = by_head(queries), by_head(keys), by_head(values)
    out = lax.map(lambda trio: attend(*(x[None] for x in trio))[0], (q_heads, k_heads, v_heads))
    out = out.reshape(per_tile, heads_local, rows_total, col_local, HEAD)
    return out.transpose(0, 2, 3, 1, 4).reshape(per_tile, rows_total, col_local, heads_local * HEAD)


def solution(mesh):
    in_specs = (
        P("groups", "tile", "chan", None),
        P(("groups", "tile"), None, "chan", None),
        P("groups"),
        P(None, None, None, "low"),
        P(None, "low"),
        P(None, None, "low"),
    )
    out_specs = P(("groups", "tile"), None, "chan", "low")
    return jax.shard_map(
        per_device, mesh=mesh, in_specs=in_specs, out_specs=out_specs, check_vma=False
    )
```

```python
import math

import jax
import jax.numpy as jnp
from jax import lax
from jax.sharding import PartitionSpec as P

HEAD = 64
TE = 256


def time_embedding(timestep):
    halfway = TE // 2
    ladder = jnp.arange(halfway, dtype=jnp.float32)
    frequency = jnp.exp(ladder * (-math.log(10000.0) / halfway))
    angles = timestep.astype(jnp.float32)[:, None] * frequency[None, :]
    return jnp.concatenate([jnp.sin(angles), jnp.cos(angles)], axis=1)


def swap(tree, axis):
    return lax.ppermute(tree, axis, [(0, 1), (1, 0)])


def convolve(joined, weight):
    return lax.conv_general_dilated(
        joined,
        weight,
        window_strides=(1, 1),
        padding=((1, 1), (1, 1)),
        dimension_numbers=("NHWC", "HWIO", "NHWC"),
        preferred_element_type=jnp.float32,
    )


def attend(queries, keys, values):
    scores = jnp.einsum("nqd,nkd->nqk", queries, keys, preferred_element_type=jnp.float32)
    scores = scores * HEAD ** (-0.5)
    row_peak = jnp.max(scores, axis=2, keepdims=True)
    weights = jnp.exp(scores - row_peak)
    totals = jnp.sum(weights, axis=2, keepdims=True)
    summed = jnp.einsum(
        "nqk,nkd->nqd", weights.astype(jnp.bfloat16), values, preferred_element_type=jnp.float32
    )
    return (summed / totals).astype(jnp.bfloat16)


def per_device(latent_map, inner_map, timestep, conv_weight, time_weight, attend_weight):
    tiles = lax.axis_size("tile")
    lows = lax.axis_size("low")
    t_idx = lax.axis_index("tile")
    c_idx = lax.axis_index("chan")
    l_idx = lax.axis_index("low")
    samples, row_local, col_local, width = latent_map.shape
    per_tile = samples // tiles
    per_core = per_tile // lows
    half = conv_weight.shape[3]
    heads_local = attend_weight.shape[2] // HEAD

    conv_other, time_other = swap((conv_weight, time_weight), "low")

    start = l_idx * per_core
    stamps = lax.dynamic_slice_in_dim(timestep, t_idx * per_tile + start, per_core, 0)
    embedded = time_embedding(stamps)
    mod_own = jnp.dot(embedded, time_weight.astype(jnp.float32), precision=lax.Precision.HIGHEST)
    mod_other = jnp.dot(embedded, time_other.astype(jnp.float32), precision=lax.Precision.HIGHEST)

    start = l_idx * per_core
    chans = lax.axis_size("chan")
    blocks = lax.dynamic_slice_in_dim(
        latent_map.reshape(tiles, per_tile, row_local, col_local, width), start, per_core, 1
    )
    inner_own = lax.dynamic_slice_in_dim(inner_map, start, per_core, 0)
    if tiles * chans <= 8 and chans == 2:
        outgoing = jnp.broadcast_to(blocks[:, None], (tiles, chans) + blocks.shape[1:])
        arrived = lax.all_to_all(
            outgoing.reshape((tiles * chans,) + blocks.shape[1:]), ("tile", "chan"), 0, 0, tiled=True
        )
        arrived = arrived.reshape(tiles, chans, per_core, row_local, col_local, width)
        latent_whole = arrived.transpose(2, 0, 3, 1, 4, 5).reshape(
            per_core, tiles * row_local, chans * col_local, width
        )
        inner_gated, mod_own, mod_other = lax.optimization_barrier((inner_own, mod_own, mod_other))
        partner = swap(inner_gated, "chan")
        inner_whole = lax.dynamic_slice_in_dim(
            jnp.concatenate([inner_own, partner, inner_own], axis=2), c_idx * col_local, 2 * col_local, 2
        )
        whole = (latent_whole.astype(jnp.float32) + inner_whole.astype(jnp.float32)).astype(jnp.bfloat16)
    else:
        outgoing = blocks.reshape(tiles * per_core, row_local, col_local, width)
        arrived = lax.all_to_all(outgoing, "tile", split_axis=0, concat_axis=1, tiled=True)
        joined = (arrived.astype(jnp.float32) + inner_own.astype(jnp.float32)).astype(jnp.bfloat16)
        whole = lax.all_gather(joined, "chan", axis=2, tiled=True)

    def features_of(weight, modulation):
        convolved = convolve(whole, weight)
        return jax.nn.silu(convolved * (1.0 + modulation[:, None, None, :])).astype(jnp.bfloat16)

    feat_own = features_of(conv_weight, mod_own)
    feat_other = features_of(conv_other, mod_other)
    nat_own = lax.dynamic_slice_in_dim(
        jnp.concatenate([feat_own, feat_other, feat_own], axis=3), l_idx * half, 2 * half, 3
    )
    nat_part = swap(nat_own, "low")
    features = lax.dynamic_slice_in_dim(
        jnp.concatenate([nat_own, nat_part, nat_own], axis=0), l_idx * per_core, per_tile, 0
    )
    rows_total, cols_total = features.shape[1], features.shape[2]
    tokens = rows_total * cols_total

    def project(part, which):
        return jnp.dot(part, attend_weight[which], preferred_element_type=jnp.float32).astype(jnp.bfloat16)

    own_cols = lax.dynamic_slice_in_dim(features, c_idx * col_local, col_local, 2)
    flat = features.reshape(per_tile, tokens, width)
    queries = project(own_cols.reshape(per_tile, -1, width), 0)
    keys = project(flat, 1)
    values = project(flat, 2)
    query_count = queries.shape[1]
    if tokens * query_count * 4 * per_tile * heads_local <= (8 << 20):
        split = lambda x: x.reshape(per_tile, x.shape[1], heads_local, HEAD)
        q4, k4, v4 = split(queries), split(keys), split(values)
        scores = jnp.einsum("bqhd,bkhd->bhqk", q4, k4, preferred_element_type=jnp.float32)
        scores = scores * HEAD ** (-0.5)
        row_peak = jnp.max(scores, axis=3, keepdims=True)
        weights = jnp.exp(scores - row_peak)
        totals = jnp.sum(weights, axis=3)
        summed = jnp.einsum(
            "bhqk,bkhd->bqhd", weights.astype(jnp.bfloat16), v4, preferred_element_type=jnp.float32
        )
        out = (summed / totals.transpose(0, 2, 1)[..., None]).astype(jnp.bfloat16)
        return out.reshape(per_tile, rows_total, col_local, heads_local * HEAD)

    def by_head(x):
        n, k, _ = x.shape
        return x.reshape(n, k, heads_local, HEAD).transpose(0, 2, 1, 3).reshape(n * heads_local, k, HEAD)

    q_heads, k_heads, v_heads = by_head(queries), by_head(keys), by_head(values)
    out = lax.map(lambda trio: attend(*(x[None] for x in trio))[0], (q_heads, k_heads, v_heads))
    out = out.reshape(per_tile, heads_local, rows_total, col_local, HEAD)
    return out.transpose(0, 2, 3, 1, 4).reshape(per_tile, rows_total, col_local, heads_local * HEAD)


def solution(mesh):
    in_specs = (
        P("groups", "tile", "chan", None),
        P(("groups", "tile"), None, "chan", None),
        P("groups"),
        P(None, None, None, "low"),
        P(None, "low"),
        P(None, None, "low"),
    )
    out_specs = P(("groups", "tile"), None, "chan", "low")
    return jax.shard_map(
        per_device, mesh=mesh, in_specs=in_specs, out_specs=out_specs, check_vma=False
    )
```

```python
import math

import jax
import jax.numpy as jnp
from jax import lax
from jax.sharding import PartitionSpec as P

HEAD = 64
TE = 256


def time_embedding(timestep):
    halfway = TE // 2
    ladder = jnp.arange(halfway, dtype=jnp.float32)
    frequency = jnp.exp(ladder * (-math.log(10000.0) / halfway))
    angles = timestep.astype(jnp.float32)[:, None] * frequency[None, :]
    return jnp.concatenate([jnp.sin(angles), jnp.cos(angles)], axis=1)


def swap(tree, axis):
    return lax.ppermute(tree, axis, [(0, 1), (1, 0)])


def convolve(joined, weight):
    return lax.conv_general_dilated(
        joined,
        weight,
        window_strides=(1, 1),
        padding=((1, 1), (1, 1)),
        dimension_numbers=("NHWC", "HWIO", "NHWC"),
        preferred_element_type=jnp.float32,
    )


def attend(queries, keys, values):
    scores = jnp.einsum("nqd,nkd->nqk", queries, keys, preferred_element_type=jnp.float32)
    scores = scores * HEAD ** (-0.5)
    row_peak = jnp.max(scores, axis=2, keepdims=True)
    weights = jnp.exp(scores - row_peak)
    totals = jnp.sum(weights, axis=2, keepdims=True)
    summed = jnp.einsum(
        "nqk,nkd->nqd", weights.astype(jnp.bfloat16), values, preferred_element_type=jnp.float32
    )
    return (summed / totals).astype(jnp.bfloat16)


def per_device(latent_map, inner_map, timestep, conv_weight, time_weight, attend_weight):
    tiles = lax.axis_size("tile")
    lows = lax.axis_size("low")
    t_idx = lax.axis_index("tile")
    c_idx = lax.axis_index("chan")
    l_idx = lax.axis_index("low")
    samples, row_local, col_local, width = latent_map.shape
    per_tile = samples // tiles
    per_core = per_tile // lows
    half = conv_weight.shape[3]
    heads_local = attend_weight.shape[2] // HEAD

    conv_other, time_other = swap((conv_weight, time_weight), "low")

    start = l_idx * per_core
    picks = t_idx * per_tile + start + jnp.arange(per_core)
    chosen = jnp.arange(samples)[None, :] == picks[:, None]
    stamps = jnp.sum(jnp.where(chosen, timestep[None, :], 0), axis=1)
    embedded = time_embedding(stamps)
    mod_own = jnp.dot(embedded, time_weight.astype(jnp.float32), precision=lax.Precision.HIGHEST)
    mod_other = jnp.dot(embedded, time_other.astype(jnp.float32), precision=lax.Precision.HIGHEST)

    start = l_idx * per_core
    chans = lax.axis_size("chan")
    blocks = lax.dynamic_slice_in_dim(
        latent_map.reshape(tiles, per_tile, row_local, col_local, width), start, per_core, 1
    )
    inner_own = lax.dynamic_slice_in_dim(inner_map, start, per_core, 0)
    if tiles * chans <= 8 and chans == 2:
        outgoing = jnp.broadcast_to(blocks[:, None], (tiles, chans) + blocks.shape[1:])
        arrived = lax.all_to_all(
            outgoing.reshape((tiles * chans,) + blocks.shape[1:]), ("tile", "chan"), 0, 0, tiled=True
        )
        arrived = arrived.reshape(tiles, chans, per_core, row_local, col_local, width)
        latent_whole = arrived.transpose(2, 0, 3, 1, 4, 5).reshape(
            per_core, tiles * row_local, chans * col_local, width
        )
        inner_gated, mod_own, mod_other = lax.optimization_barrier((inner_own, mod_own, mod_other))
        partner = swap(inner_gated, "chan")
        inner_whole = lax.dynamic_slice_in_dim(
            jnp.concatenate([inner_own, partner, inner_own], axis=2), c_idx * col_local, 2 * col_local, 2
        )
        whole = (latent_whole.astype(jnp.float32) + inner_whole.astype(jnp.float32)).astype(jnp.bfloat16)
    else:
        outgoing = blocks.reshape(tiles * per_core, row_local, col_local, width)
        arrived = lax.all_to_all(outgoing, "tile", split_axis=0, concat_axis=1, tiled=True)
        joined = (arrived.astype(jnp.float32) + inner_own.astype(jnp.float32)).astype(jnp.bfloat16)
        whole = lax.all_gather(joined, "chan", axis=2, tiled=True)

    def features_of(weight, modulation):
        convolved = convolve(whole, weight)
        return jax.nn.silu(convolved * (1.0 + modulation[:, None, None, :])).astype(jnp.bfloat16)

    feat_own = features_of(conv_weight, mod_own)
    feat_other = features_of(conv_other, mod_other)
    nat_own = lax.dynamic_slice_in_dim(
        jnp.concatenate([feat_own, feat_other, feat_own], axis=3), l_idx * half, 2 * half, 3
    )
    nat_part = swap(nat_own, "low")
    features = lax.dynamic_slice_in_dim(
        jnp.concatenate([nat_own, nat_part, nat_own], axis=0), l_idx * per_core, per_tile, 0
    )
    rows_total, cols_total = features.shape[1], features.shape[2]
    tokens = rows_total * cols_total

    def project(part, which):
        return jnp.dot(part, attend_weight[which], preferred_element_type=jnp.float32).astype(jnp.bfloat16)

    own_cols = lax.dynamic_slice_in_dim(features, c_idx * col_local, col_local, 2)
    flat = features.reshape(per_tile, tokens, width)
    queries = project(own_cols.reshape(per_tile, -1, width), 0)
    keys = project(flat, 1)
    values = project(flat, 2)
    query_count = queries.shape[1]
    if tokens * query_count * 4 * per_tile * heads_local <= (8 << 20):
        split = lambda x: x.reshape(per_tile, x.shape[1], heads_local, HEAD)
        q4, k4, v4 = split(queries), split(keys), split(values)
        scores = jnp.einsum("bqhd,bkhd->bhqk", q4, k4, preferred_element_type=jnp.float32)
        scores = scores * HEAD ** (-0.5)
        row_peak = jnp.max(scores, axis=3, keepdims=True)
        weights = jnp.exp(scores - row_peak)
        totals = jnp.sum(weights, axis=3)
        summed = jnp.einsum(
            "bhqk,bkhd->bqhd", weights.astype(jnp.bfloat16), v4, preferred_element_type=jnp.float32
        )
        out = (summed / totals.transpose(0, 2, 1)[..., None]).astype(jnp.bfloat16)
        return out.reshape(per_tile, rows_total, col_local, heads_local * HEAD)

    def by_head(x):
        n, k, _ = x.shape
        return x.reshape(n, k, heads_local, HEAD).transpose(0, 2, 1, 3).reshape(n * heads_local, k, HEAD)

    q_heads, k_heads, v_heads = by_head(queries), by_head(keys), by_head(values)
    out = lax.map(lambda trio: attend(*(x[None] for x in trio))[0], (q_heads, k_heads, v_heads))
    out = out.reshape(per_tile, heads_local, rows_total, col_local, HEAD)
    return out.transpose(0, 2, 3, 1, 4).reshape(per_tile, rows_total, col_local, heads_local * HEAD)


def solution(mesh):
    in_specs = (
        P("groups", "tile", "chan", None),
        P(("groups", "tile"), None, "chan", None),
        P("groups"),
        P(None, None, None, "low"),
        P(None, "low"),
        P(None, None, "low"),
    )
    out_specs = P(("groups", "tile"), None, "chan", "low")
    return jax.shard_map(
        per_device, mesh=mesh, in_specs=in_specs, out_specs=out_specs, check_vma=False
    )
```

```python
import math

import jax
import jax.numpy as jnp
from jax import lax
from jax.sharding import PartitionSpec as P

HEAD = 64
TE = 256


def time_embedding(timestep):
    halfway = TE // 2
    ladder = jnp.arange(halfway, dtype=jnp.float32)
    frequency = jnp.exp(ladder * (-math.log(10000.0) / halfway))
    angles = timestep.astype(jnp.float32)[:, None] * frequency[None, :]
    return jnp.concatenate([jnp.sin(angles), jnp.cos(angles)], axis=1)


def swap(tree, axis):
    return lax.ppermute(tree, axis, [(0, 1), (1, 0)])


def convolve(joined, weight):
    return lax.conv_general_dilated(
        joined,
        weight,
        window_strides=(1, 1),
        padding=((1, 1), (1, 1)),
        dimension_numbers=("NHWC", "HWIO", "NHWC"),
        preferred_element_type=jnp.float32,
    )


def attend(queries, keys, values):
    scores = jnp.einsum("nqd,nkd->nqk", queries, keys, preferred_element_type=jnp.float32)
    scores = scores * HEAD ** (-0.5)
    row_peak = jnp.max(scores, axis=2, keepdims=True)
    weights = jnp.exp(scores - row_peak)
    totals = jnp.sum(weights, axis=2, keepdims=True)
    summed = jnp.einsum(
        "nqk,nkd->nqd", weights.astype(jnp.bfloat16), values, preferred_element_type=jnp.float32
    )
    return (summed / totals).astype(jnp.bfloat16)


def per_device(latent_map, inner_map, timestep, conv_weight, time_weight, attend_weight):
    tiles = lax.axis_size("tile")
    lows = lax.axis_size("low")
    t_idx = lax.axis_index("tile")
    c_idx = lax.axis_index("chan")
    l_idx = lax.axis_index("low")
    samples, row_local, col_local, width = latent_map.shape
    per_tile = samples // tiles
    per_core = per_tile // lows
    half = conv_weight.shape[3]
    heads_local = attend_weight.shape[2] // HEAD

    conv_other, time_other = swap((conv_weight, time_weight), "low")

    start = l_idx * per_core
    stamps = lax.dynamic_slice_in_dim(timestep, t_idx * per_tile + start, per_core, 0)
    embedded = time_embedding(stamps)
    mod_own = jnp.dot(embedded, time_weight.astype(jnp.float32), precision=lax.Precision.HIGHEST)
    mod_other = jnp.dot(embedded, time_other.astype(jnp.float32), precision=lax.Precision.HIGHEST)

    start = l_idx * per_core
    chans = lax.axis_size("chan")
    blocks = lax.dynamic_slice_in_dim(
        latent_map.reshape(tiles, per_tile, row_local, col_local, width), start, per_core, 1
    )
    inner_own = lax.dynamic_slice_in_dim(inner_map, start, per_core, 0)
    if tiles * chans <= 8 and chans == 2:
        outgoing = jnp.broadcast_to(blocks[None], (chans,) + blocks.shape)
        arrived = lax.all_to_all(
            outgoing.reshape((chans * tiles,) + blocks.shape[1:]), ("chan", "tile"), 0, 0, tiled=True
        )
        arrived = arrived.reshape(chans, tiles, per_core, row_local, col_local, width)
        latent_whole = arrived.transpose(2, 1, 3, 0, 4, 5).reshape(
            per_core, tiles * row_local, chans * col_local, width
        )
        inner_gated, mod_own, mod_other = lax.optimization_barrier((inner_own, mod_own, mod_other))
        partner = swap(inner_gated, "chan")
        inner_whole = lax.dynamic_slice_in_dim(
            jnp.concatenate([inner_own, partner, inner_own], axis=2), c_idx * col_local, 2 * col_local, 2
        )
        whole = (latent_whole.astype(jnp.float32) + inner_whole.astype(jnp.float32)).astype(jnp.bfloat16)
    else:
        outgoing = blocks.reshape(tiles * per_core, row_local, col_local, width)
        arrived = lax.all_to_all(outgoing, "tile", split_axis=0, concat_axis=1, tiled=True)
        joined = (arrived.astype(jnp.float32) + inner_own.astype(jnp.float32)).astype(jnp.bfloat16)
        whole = lax.all_gather(joined, "chan", axis=2, tiled=True)

    def features_of(weight, modulation):
        convolved = convolve(whole, weight)
        return jax.nn.silu(convolved * (1.0 + modulation[:, None, None, :])).astype(jnp.bfloat16)

    feat_own = features_of(conv_weight, mod_own)
    feat_other = features_of(conv_other, mod_other)
    nat_own = lax.dynamic_slice_in_dim(
        jnp.concatenate([feat_own, feat_other, feat_own], axis=3), l_idx * half, 2 * half, 3
    )
    nat_part = swap(nat_own, "low")
    features = lax.dynamic_slice_in_dim(
        jnp.concatenate([nat_own, nat_part, nat_own], axis=0), l_idx * per_core, per_tile, 0
    )
    rows_total, cols_total = features.shape[1], features.shape[2]
    tokens = rows_total * cols_total

    def project(part, which):
        return jnp.dot(part, attend_weight[which], preferred_element_type=jnp.float32).astype(jnp.bfloat16)

    own_cols = lax.dynamic_slice_in_dim(features, c_idx * col_local, col_local, 2)
    flat = features.reshape(per_tile, tokens, width)
    queries = project(own_cols.reshape(per_tile, -1, width), 0)
    keys = project(flat, 1)
    values = project(flat, 2)
    query_count = queries.shape[1]
    if tokens * query_count * 4 * per_tile * heads_local <= (8 << 20):
        split = lambda x: x.reshape(per_tile, x.shape[1], heads_local, HEAD)
        q4, k4, v4 = split(queries), split(keys), split(values)
        scores = jnp.einsum("bqhd,bkhd->bhqk", q4, k4, preferred_element_type=jnp.float32)
        scores = scores * HEAD ** (-0.5)
        row_peak = jnp.max(scores, axis=3, keepdims=True)
        weights = jnp.exp(scores - row_peak)
        totals = jnp.sum(weights, axis=3)
        summed = jnp.einsum(
            "bhqk,bkhd->bqhd", weights.astype(jnp.bfloat16), v4, preferred_element_type=jnp.float32
        )
        out = (summed / totals.transpose(0, 2, 1)[..., None]).astype(jnp.bfloat16)
        return out.reshape(per_tile, rows_total, col_local, heads_local * HEAD)

    def by_head(x):
        n, k, _ = x.shape
        return x.reshape(n, k, heads_local, HEAD).transpose(0, 2, 1, 3).reshape(n * heads_local, k, HEAD)

    q_heads, k_heads, v_heads = by_head(queries), by_head(keys), by_head(values)
    out = lax.map(lambda trio: attend(*(x[None] for x in trio))[0], (q_heads, k_heads, v_heads))
    out = out.reshape(per_tile, heads_local, rows_total, col_local, HEAD)
    return out.transpose(0, 2, 3, 1, 4).reshape(per_tile, rows_total, col_local, heads_local * HEAD)


def solution(mesh):
    in_specs = (
        P("groups", "tile", "chan", None),
        P(("groups", "tile"), None, "chan", None),
        P("groups"),
        P(None, None, None, "low"),
        P(None, "low"),
        P(None, None, "low"),
    )
    out_specs = P(("groups", "tile"), None, "chan", "low")
    return jax.shard_map(
        per_device, mesh=mesh, in_specs=in_specs, out_specs=out_specs, check_vma=False
    )
```

```python
import math

import jax
import jax.numpy as jnp
from jax import lax
from jax.sharding import PartitionSpec as P

HEAD = 64
TE = 256


def time_embedding(timestep):
    halfway = TE // 2
    ladder = jnp.arange(halfway, dtype=jnp.float32)
    frequency = jnp.exp(ladder * (-math.log(10000.0) / halfway))
    angles = timestep.astype(jnp.float32)[:, None] * frequency[None, :]
    return jnp.concatenate([jnp.sin(angles), jnp.cos(angles)], axis=1)


def swap(tree, axis):
    return lax.ppermute(tree, axis, [(0, 1), (1, 0)])


def convolve(joined, weight):
    return lax.conv_general_dilated(
        joined,
        weight,
        window_strides=(1, 1),
        padding=((1, 1), (1, 1)),
        dimension_numbers=("NHWC", "HWIO", "NHWC"),
        preferred_element_type=jnp.float32,
    )


def attend(queries, keys, values):
    scores = jnp.einsum("nqd,nkd->nqk", queries, keys, preferred_element_type=jnp.float32)
    scores = scores * HEAD ** (-0.5)
    row_peak = jnp.max(scores, axis=2, keepdims=True)
    weights = jnp.exp(scores - row_peak)
    totals = jnp.sum(weights, axis=2, keepdims=True)
    summed = jnp.einsum(
        "nqk,nkd->nqd", weights.astype(jnp.bfloat16), values, preferred_element_type=jnp.float32
    )
    return (summed / totals).astype(jnp.bfloat16)


def per_device(latent_map, inner_map, timestep, conv_weight, time_weight, attend_weight):
    tiles = lax.axis_size("tile")
    lows = lax.axis_size("low")
    t_idx = lax.axis_index("tile")
    c_idx = lax.axis_index("chan")
    l_idx = lax.axis_index("low")
    samples, row_local, col_local, width = latent_map.shape
    per_tile = samples // tiles
    per_core = per_tile // lows
    half = conv_weight.shape[3]
    heads_local = attend_weight.shape[2] // HEAD

    conv_other, time_other = swap((conv_weight, time_weight), "low")

    start = l_idx * per_core
    stamps = lax.dynamic_slice_in_dim(timestep, t_idx * per_tile + start, per_core, 0)
    embedded = time_embedding(stamps)
    mod_own = jnp.dot(embedded, time_weight.astype(jnp.float32), precision=lax.Precision.HIGHEST)
    mod_other = jnp.dot(embedded, time_other.astype(jnp.float32), precision=lax.Precision.HIGHEST)

    start = l_idx * per_core
    chans = lax.axis_size("chan")
    blocks = lax.dynamic_slice_in_dim(
        latent_map.reshape(tiles, per_tile, row_local, col_local, width), start, per_core, 1
    )
    inner_own = lax.dynamic_slice_in_dim(inner_map, start, per_core, 0)
    if tiles * chans <= 8 and chans == 2:
        outgoing = jnp.broadcast_to(blocks[:, None], (tiles, chans) + blocks.shape[1:])
        arrived = lax.all_to_all(
            outgoing.reshape((tiles * chans,) + blocks.shape[1:]), ("tile", "chan"), 0, 0, tiled=True
        )
        arrived = arrived.reshape(tiles, chans, per_core, row_local, col_local, width)
        latent_whole = arrived.transpose(2, 0, 3, 1, 4, 5).reshape(
            per_core, tiles * row_local, chans * col_local, width
        )
        inner_gated, mod_own, mod_other = lax.optimization_barrier((inner_own, mod_own, mod_other))
        partner = swap(inner_gated, "chan")
        inner_whole = lax.dynamic_slice_in_dim(
            jnp.concatenate([inner_own, partner, inner_own], axis=2), c_idx * col_local, 2 * col_local, 2
        )
        whole = (latent_whole.astype(jnp.float32) + inner_whole.astype(jnp.float32)).astype(jnp.bfloat16)
    else:
        outgoing = blocks.reshape(tiles * per_core, row_local, col_local, width)
        arrived = lax.all_to_all(outgoing, "tile", split_axis=0, concat_axis=1, tiled=True)
        joined = (arrived.astype(jnp.float32) + inner_own.astype(jnp.float32)).astype(jnp.bfloat16)
        whole = lax.all_gather(joined, "chan", axis=2, tiled=True)

    def features_of(weight, modulation):
        convolved = convolve(whole, weight)
        return jax.nn.silu(convolved * (1.0 + modulation[:, None, None, :])).astype(jnp.bfloat16)

    feat_own = features_of(conv_weight, mod_own)
    feat_other = features_of(conv_other, mod_other)
    nat_own = lax.dynamic_slice_in_dim(
        jnp.concatenate([feat_own, feat_other, feat_own], axis=3), l_idx * half, 2 * half, 3
    )
    nat_part = swap(nat_own, "low")
    rows_total, cols_total = nat_own.shape[1], nat_own.shape[2]
    tokens = rows_total * cols_total

    def project(part, which):
        return jnp.dot(part, attend_weight[which], preferred_element_type=jnp.float32).astype(jnp.bfloat16)

    def project_sample(sample_features):
        own_cols = lax.dynamic_slice_in_dim(sample_features, c_idx * col_local, col_local, 2)
        flat = sample_features.reshape(per_core, tokens, width)
        return (
            project(own_cols.reshape(per_core, -1, width), 0),
            project(flat, 1),
            project(flat, 2),
        )

    mine, theirs = project_sample(nat_own), project_sample(nat_part)

    def in_order(pair):
        return lax.dynamic_slice_in_dim(jnp.concatenate([pair[0], pair[1], pair[0]], axis=0), l_idx * per_core, per_tile, 0)

    queries, keys, values = (in_order(pair) for pair in zip(mine, theirs))
    query_count = queries.shape[1]
    if tokens * query_count * 4 * per_tile * heads_local <= (8 << 20):
        split = lambda x: x.reshape(per_tile, x.shape[1], heads_local, HEAD)
        q4, k4, v4 = split(queries), split(keys), split(values)
        scores = jnp.einsum("bqhd,bkhd->bhqk", q4, k4, preferred_element_type=jnp.float32)
        scores = scores * HEAD ** (-0.5)
        row_peak = jnp.max(scores, axis=3, keepdims=True)
        weights = jnp.exp(scores - row_peak)
        totals = jnp.sum(weights, axis=3)
        summed = jnp.einsum(
            "bhqk,bkhd->bqhd", weights.astype(jnp.bfloat16), v4, preferred_element_type=jnp.float32
        )
        out = (summed / totals.transpose(0, 2, 1)[..., None]).astype(jnp.bfloat16)
        return out.reshape(per_tile, rows_total, col_local, heads_local * HEAD)

    def by_head(x):
        n, k, _ = x.shape
        return x.reshape(n, k, heads_local, HEAD).transpose(0, 2, 1, 3).reshape(n * heads_local, k, HEAD)

    q_heads, k_heads, v_heads = by_head(queries), by_head(keys), by_head(values)
    out = lax.map(lambda trio: attend(*(x[None] for x in trio))[0], (q_heads, k_heads, v_heads))
    out = out.reshape(per_tile, heads_local, rows_total, col_local, HEAD)
    return out.transpose(0, 2, 3, 1, 4).reshape(per_tile, rows_total, col_local, heads_local * HEAD)


def solution(mesh):
    in_specs = (
        P("groups", "tile", "chan", None),
        P(("groups", "tile"), None, "chan", None),
        P("groups"),
        P(None, None, None, "low"),
        P(None, "low"),
        P(None, None, "low"),
    )
    out_specs = P(("groups", "tile"), None, "chan", "low")
    return jax.shard_map(
        per_device, mesh=mesh, in_specs=in_specs, out_specs=out_specs, check_vma=False
    )
```

```python
import math

import jax
import jax.numpy as jnp
from jax import lax
from jax.sharding import PartitionSpec as P

HEAD = 64
TE = 256


def time_embedding(timestep):
    halfway = TE // 2
    ladder = jnp.arange(halfway, dtype=jnp.float32)
    frequency = jnp.exp(ladder * (-math.log(10000.0) / halfway))
    angles = timestep.astype(jnp.float32)[:, None] * frequency[None, :]
    return jnp.concatenate([jnp.sin(angles), jnp.cos(angles)], axis=1)


def swap(tree, axis):
    return lax.ppermute(tree, axis, [(0, 1), (1, 0)])


def convolve(joined, weight):
    return lax.conv_general_dilated(
        joined,
        weight,
        window_strides=(1, 1),
        padding=((1, 1), (1, 1)),
        dimension_numbers=("NHWC", "HWIO", "NHWC"),
        preferred_element_type=jnp.float32,
    )


def attend(queries, keys, values):
    scores = jnp.einsum("nqd,nkd->nqk", queries, keys, preferred_element_type=jnp.float32)
    scores = scores * HEAD ** (-0.5)
    row_peak = jnp.max(scores, axis=2, keepdims=True)
    weights = jnp.exp(scores - row_peak)
    totals = jnp.sum(weights, axis=2, keepdims=True)
    summed = jnp.einsum(
        "nqk,nkd->nqd", weights.astype(jnp.bfloat16), values, preferred_element_type=jnp.float32
    )
    return (summed / totals).astype(jnp.bfloat16)


def per_device(latent_map, inner_map, timestep, conv_weight, time_weight, attend_weight):
    tiles = lax.axis_size("tile")
    lows = lax.axis_size("low")
    t_idx = lax.axis_index("tile")
    c_idx = lax.axis_index("chan")
    l_idx = lax.axis_index("low")
    samples, row_local, col_local, width = latent_map.shape
    per_tile = samples // tiles
    per_core = per_tile // lows
    half = conv_weight.shape[3]
    heads_local = attend_weight.shape[2] // HEAD

    conv_other, time_other = swap((conv_weight, time_weight), "low")

    start = l_idx * per_core
    stamps = lax.dynamic_slice_in_dim(timestep, t_idx * per_tile + start, per_core, 0)
    embedded = time_embedding(stamps)
    mod_own = jnp.dot(embedded, time_weight.astype(jnp.float32), precision=lax.Precision.HIGHEST)
    mod_other = jnp.dot(embedded, time_other.astype(jnp.float32), precision=lax.Precision.HIGHEST)

    start = l_idx * per_core
    chans = lax.axis_size("chan")
    blocks = lax.dynamic_slice_in_dim(
        latent_map.reshape(tiles, per_tile, row_local, col_local, width), start, per_core, 1
    )
    inner_own = lax.dynamic_slice_in_dim(inner_map, start, per_core, 0)
    if tiles * chans <= 8 and chans == 2:
        outgoing = jnp.broadcast_to(blocks[:, None], (tiles, chans) + blocks.shape[1:])
        arrived = lax.all_to_all(
            outgoing.reshape((tiles * chans,) + blocks.shape[1:]), ("tile", "chan"), 0, 0, tiled=True
        )
        arrived = arrived.reshape(tiles, chans, per_core, row_local, col_local, width)
        latent_whole = arrived.transpose(2, 0, 3, 1, 4, 5).reshape(
            per_core, tiles * row_local, chans * col_local, width
        )
        inner_gated, mod_own, mod_other = lax.optimization_barrier((inner_own, mod_own, mod_other))
        partner = swap(inner_gated, "chan")
        inner_whole = lax.dynamic_slice_in_dim(
            jnp.concatenate([inner_own, partner, inner_own], axis=2), c_idx * col_local, 2 * col_local, 2
        )
        whole = (latent_whole.astype(jnp.float32) + inner_whole.astype(jnp.float32)).astype(jnp.bfloat16)
    else:
        outgoing = blocks.reshape(tiles * per_core, row_local, col_local, width)
        arrived = lax.all_to_all(outgoing, "tile", split_axis=0, concat_axis=1, tiled=True)
        joined = (arrived.astype(jnp.float32) + inner_own.astype(jnp.float32)).astype(jnp.bfloat16)
        whole = lax.all_gather(joined, "chan", axis=2, tiled=True)

    def features_of(weight, modulation):
        convolved = convolve(whole, weight)
        return jax.nn.silu(convolved * (1.0 + modulation[:, None, None, :])).astype(jnp.bfloat16)

    feat_own = features_of(conv_weight, mod_own)
    feat_other = features_of(conv_other, mod_other)
    nat_own = lax.dynamic_slice_in_dim(
        jnp.concatenate([feat_own, feat_other, feat_own], axis=3), l_idx * half, 2 * half, 3
    )
    nat_part = swap(nat_own, "low")
    features = lax.dynamic_slice_in_dim(
        jnp.concatenate([nat_own, nat_part, nat_own], axis=0), l_idx * per_core, per_tile, 0
    )
    rows_total, cols_total = features.shape[1], features.shape[2]
    tokens = rows_total * cols_total

    def project(part, which):
        return jnp.dot(part, attend_weight[which], preferred_element_type=jnp.float32).astype(jnp.bfloat16)

    own_cols = lax.dynamic_slice_in_dim(features, c_idx * col_local, col_local, 2)
    flat = features.reshape(per_tile, tokens, width)
    queries = project(own_cols.reshape(per_tile, -1, width), 0)
    pair_weight = jnp.concatenate([attend_weight[1], attend_weight[2]], axis=1)
    both = jnp.dot(flat, pair_weight, preferred_element_type=jnp.float32).astype(jnp.bfloat16)
    keys, values = both[..., :half], both[..., half:]
    query_count = queries.shape[1]
    if tokens * query_count * 4 * per_tile * heads_local <= (8 << 20):
        split = lambda x: x.reshape(per_tile, x.shape[1], heads_local, HEAD)
        q4, k4, v4 = split(queries), split(keys), split(values)
        scores = jnp.einsum("bqhd,bkhd->bhqk", q4, k4, preferred_element_type=jnp.float32)
        scores = scores * HEAD ** (-0.5)
        row_peak = jnp.max(scores, axis=3, keepdims=True)
        weights = jnp.exp(scores - row_peak)
        totals = jnp.sum(weights, axis=3)
        summed = jnp.einsum(
            "bhqk,bkhd->bqhd", weights.astype(jnp.bfloat16), v4, preferred_element_type=jnp.float32
        )
        out = (summed / totals.transpose(0, 2, 1)[..., None]).astype(jnp.bfloat16)
        return out.reshape(per_tile, rows_total, col_local, heads_local * HEAD)

    def by_head(x):
        n, k, _ = x.shape
        return x.reshape(n, k, heads_local, HEAD).transpose(0, 2, 1, 3).reshape(n * heads_local, k, HEAD)

    q_heads, k_heads, v_heads = by_head(queries), by_head(keys), by_head(values)
    out = lax.map(lambda trio: attend(*(x[None] for x in trio))[0], (q_heads, k_heads, v_heads))
    out = out.reshape(per_tile, heads_local, rows_total, col_local, HEAD)
    return out.transpose(0, 2, 3, 1, 4).reshape(per_tile, rows_total, col_local, heads_local * HEAD)


def solution(mesh):
    in_specs = (
        P("groups", "tile", "chan", None),
        P(("groups", "tile"), None, "chan", None),
        P("groups"),
        P(None, None, None, "low"),
        P(None, "low"),
        P(None, None, "low"),
    )
    out_specs = P(("groups", "tile"), None, "chan", "low")
    return jax.shard_map(
        per_device, mesh=mesh, in_specs=in_specs, out_specs=out_specs, check_vma=False
    )
```
